512 devices in a mesh: dp: 128 (over y, z, core), mp: 4 (over x).
Axes of the slice: x: 4, y: 8, z: 8, core: 2. Of those that a mesh axis runs over, the one named last changes fastest.
Arguments:
- frames: bfloat16 [262144, 320], P('dp'), may hold values from -6 to 6
- lengths: int32 [128, 256], P('dp'), may hold values from 0 to 15, as said below
- destinations: int32 [128, 256], P('dp'), may hold values from 0 to 127, as said below
- offsets: int32 [128, 256], P('dp'), may hold values from 0 to 255, as said below
- in_weight: bfloat16 [320, 1536], P(None, 'mp'), may hold values from -0.3125 to 0.3125
- depth_weight: bfloat16 [31, 1536], P(None, 'mp'), may hold values from -1 to 1
- out_weight: bfloat16 [1536, 1536], P(None, 'mp'), may hold values from -0.15625 to 0.15625
- cotangent: bfloat16 [32768, 1536], P('dp', 'mp'), may hold values from -24 to 24
Outputs:
- output: bfloat16 [32768, 1536], P('dp', 'mp')
- in_weight_gradient: float32 [320, 1536], P(None, 'mp')
- depth_gradient: float32 [31, 1536], P(None, 'mp')
- out_weight_gradient: float32 [1536, 1536], P('dp', 'mp')
The draws below stay inside these ranges and needn't reach their ends.
Inputs may be any that keep to these rules, and one draw needn't show every extreme that they name: Used entries of a device's list come first and have lengths of 1 or more; later entries have length 0; some utterance has exactly 15 rows. `destinations`: A device's utterances for one destination stand together and fill exactly 16 rows; unused entries name device 0; some device sends to every device. `offsets`: the utterances sent to one device tile its 256 rows exactly; unused entries have offset 0; on every device some utterance starts at row 255.
All inputs are finite; a program needn't handle non-finite values.
Results may differ from the reference program's by a relative error of at most 0.014.
Values may be sent and summed in bfloat16 or wider, within the bound.
No kernel may reach another device: no remote copies, remote signals or barrier semaphores. Data moves between devices by JAX's collectives and lax.ppermute only.
A program may use at most 64 MiB of HBM per device.

```python
import math
import jax
import jax.numpy as jnp
from jax import lax

D = 1536
FEAT = 320
KERNEL = 31
PAIR_ROWS = 16
PAIRS = 16
ROWS = 256
SOURCE_ROW_COUNT = 2048
TOKENS = 32768
N_DP = 128
N_MP = 4


def routing_tables(key):
    base_key = jax.random.fold_in(key, 11)
    ranking_key, heavy_key, length_key = jax.random.split(base_key, 3)
    sources = min(PAIRS, N_DP // 4)
    per_slot = PAIRS // sources
    entries = 2 * N_DP * per_slot
    device_numbers = jnp.arange(N_DP, dtype=jnp.int32)
    ordering_numbers = jax.random.permutation(heavy_key, N_DP)
    extra_rank_order = jnp.where(device_numbers == 0, 2 ** 23, jnp.where(device_numbers <= N_DP // 8, 2 ** 19, 0)).astype(jnp.int32)
    extra_score_values = jnp.zeros((N_DP,), jnp.int32).at[ordering_numbers].set(extra_rank_order)
    priority_scores = jax.random.randint(ranking_key, (N_DP, N_DP), 0, 2 ** 20, dtype=jnp.int32) + extra_score_values[None, :]
    priority_scores = priority_scores * N_DP + device_numbers[None, :]
    chosen = lax.top_k(priority_scores, sources)[1].astype(jnp.int32)
    first_part = jax.random.randint(length_key, (N_DP, PAIRS), 1, PAIR_ROWS, dtype=jnp.int32)
    first_part = first_part.at[:, 0].set(1)
    first_part = first_part.at[:, PAIRS - 1].set(PAIR_ROWS - 1)
    chosen_mask = jnp.zeros((N_DP, N_DP), jnp.int32).at[device_numbers[:, None], chosen].set(1)
    rank_table = jnp.cumsum(chosen_mask, axis=0, dtype=jnp.int32) - 1
    grid_shape = (N_DP, sources, per_slot, 2)
    dest_grid = jnp.broadcast_to(device_numbers[:, None, None, None], grid_shape)
    slot_grid = jnp.broadcast_to(jnp.arange(sources, dtype=jnp.int32)[None, :, None, None], grid_shape)
    inner_pair = jnp.broadcast_to(jnp.arange(per_slot, dtype=jnp.int32)[None, None, :, None], grid_shape)
    member_side = jnp.broadcast_to(jnp.arange(2, dtype=jnp.int32)[None, None, None, :], grid_shape)
    source_grid = jnp.broadcast_to(chosen[:, :, None, None], grid_shape)
    rank_grid = rank_table[dest_grid, source_grid]
    pair_index = slot_grid * per_slot + inner_pair
    entry_index = (rank_grid * per_slot + inner_pair) * 2 + member_side
    first_len = first_part[dest_grid, pair_index]
    length_grid = jnp.where(member_side == 0, first_len, PAIR_ROWS - first_len).astype(jnp.int32)
    offset_grid = (pair_index * PAIR_ROWS + member_side * first_len).astype(jnp.int32)
    empty_table = jnp.zeros((N_DP, entries), jnp.int32)
    lengths = empty_table.at[source_grid, entry_index].set(length_grid)
    destinations = empty_table.at[source_grid, entry_index].set(dest_grid)
    offsets = empty_table.at[source_grid, entry_index].set(offset_grid)
    return (lengths, destinations, offsets)


def draw_lengths(key, part):
    return routing_tables(key)[0]


def draw_destinations(key, part):
    return routing_tables(key)[1]


def draw_offsets(key, part):
    return routing_tables(key)[2]


def with_spikes(values, stream_key, source, target, parts, factor):
    owner, partner = [(jnp.arange(values.shape[position]) // (values.shape[position] // parts)).reshape([-1 if axis == position else 1 for axis in range(values.ndim)]) for position in (source, target)]
    chosen = jax.random.permutation(stream_key, parts)[partner]
    strong = (owner == chosen) | (owner == (partner + parts // 2) % parts)
    return jnp.where(strong, factor * values, values)


def level_of(stream_key, dims, cuts, least, high):
    def one(position, parts):
        heights = jax.random.uniform(jax.random.fold_in(jax.random.fold_in(stream_key, 6), position), (parts,), jnp.float32, least / len(cuts), high / len(cuts))
        return jnp.repeat(jnp.exp(heights), dims[position] // parts).reshape((-1,) + (1,) * (len(dims) - position - 1))

    factor_of = one(*cuts[0])
    for cut in cuts[1:]:
        factor_of = factor_of * one(*cut)
    return factor_of


def scatter_about(stream_key, dims, deviation, reach, cuts=(), kind=jnp.bfloat16):
    gain = level_of(stream_key, dims, cuts, -0.22, 0.18) if cuts else 1.0
    values = jax.random.normal(stream_key, dims, jnp.float32) * deviation * gain
    return jnp.minimum(jnp.maximum(values, -reach), reach).astype(kind)


def noise_with(own_key, extent, width, limit, shards, heavy, kind=jnp.bfloat16):
    values = width * jax.random.normal(own_key, extent, jnp.float32)
    if shards:
        values = values * level_of(own_key, extent, shards, -0.22, 0.18)
    return jnp.clip(with_spikes(values, jax.random.fold_in(own_key, 3), *heavy), -limit, limit).astype(kind)


def setup_inputs(seed: int = 0) -> dict:
    splits = jax.random.split(jax.random.key(seed), 9)
    return {
        "frames": scatter_about(splits[0], (N_DP * SOURCE_ROW_COUNT, FEAT), 1.0, 6.0, ((0, 128),)),
        "lengths": draw_lengths(jax.random.fold_in(splits[8], 71), 0),
        "destinations": draw_destinations(jax.random.fold_in(splits[8], 71), 0),
        "offsets": draw_offsets(jax.random.fold_in(splits[8], 71), 0),
        "in_weight": scatter_about(splits[4], (FEAT, D), FEAT ** -0.5, 0.3125, ((1, 4),)),
        "depth_weight": scatter_about(splits[5], (KERNEL, D), KERNEL ** -0.5, 1.0, ((1, 4),)),
        "out_weight": scatter_about(splits[6], (D, D), D ** -0.5, 0.15625, ((1, 4),)),
        "cotangent": noise_with(splits[7], (TOKENS, D), 1.0, 24.0, ((0, 128), (1, 4)), (0, 1, 128, 5.5)),
    }


def depth_conv(values, weights, labels, direction):
    center = (KERNEL - 1) // 2
    length = values.shape[0]
    padded = jnp.pad(values, ((center, center), (0, 0)))
    padded_labels = jnp.pad(labels, (center, center), constant_values=-1)
    result = jnp.zeros(values.shape, jnp.float32)
    for tap_index in range(KERNEL):
        start = center + direction * (tap_index - center)
        matches = (padded_labels[start:start + length] == labels)[:, None]
        taken = weights[tap_index][None, :] * padded[start:start + length]
        result = result + jnp.where(matches, taken, jnp.zeros_like(taken))
    return result

def tap_sums(grads, values, labels):
    center = (KERNEL - 1) // 2
    length = values.shape[0]
    padded = jnp.pad(values, ((center, center), (0, 0)))
    padded_labels = jnp.pad(labels, (center, center), constant_values=-1)
    rows_list = []
    for tap_index in range(KERNEL):
        start = tap_index
        matches = (padded_labels[start:start + length] == labels)[:, None]
        taken = grads * padded[start:start + length]
        rows_list.append(lax.optimization_barrier(jnp.sum(jnp.where(matches, taken, jnp.zeros_like(taken)), axis=0)))
    return jnp.stack(rows_list, 0)

def source_targets(items):
    lengths_row, dests_row, offsets_row, source = items
    entries = lengths_row.shape[0]
    end_rows = jnp.cumsum(lengths_row, dtype=jnp.int32)
    begins = end_rows - lengths_row
    row_ids = jnp.arange(SOURCE_ROW_COUNT, dtype=jnp.int32)
    owner_index = lax.optimization_barrier(jnp.sum((end_rows[None, :] <= row_ids[:, None]).astype(jnp.int32), axis=1, dtype=jnp.int32))
    occupied_rows = owner_index < entries
    clamped = jnp.minimum(owner_index, entries - 1).astype(jnp.int32)
    target = dests_row[clamped] * ROWS + offsets_row[clamped] + row_ids - begins[clamped]
    target = jnp.where(occupied_rows, target, N_DP * ROWS).astype(jnp.int32)
    row_label = (source * entries + clamped).astype(jnp.int32)
    return (target, row_label)

def reference(frames, lengths, destinations, offsets, in_weight, depth_weight, out_weight, cotangent):
    all_rows = N_DP * ROWS
    device_numbers = jnp.arange(N_DP, dtype=jnp.int32)
    targets, labels = lax.map(source_targets, (lengths, destinations, offsets, device_numbers))
    flat_targets = targets.reshape(-1)
    packed = jnp.zeros((all_rows + 1, FEAT), frames.dtype).at[flat_targets].set(frames)[:all_rows]
    packed_labels = jnp.full((all_rows + 1,), -1, jnp.int32).at[flat_targets].set(labels.reshape(-1))[:all_rows]
    hidden = jnp.dot(packed, in_weight, preferred_element_type=jnp.float32).astype(jnp.bfloat16)
    hidden_wide = hidden.astype(jnp.float32)
    taps = depth_weight.astype(jnp.float32)
    convolved = depth_conv(hidden_wide, taps, packed_labels, 1)
    activated = jax.nn.silu(convolved).astype(jnp.bfloat16)
    shard_width = D // N_MP
    branch = jnp.zeros((all_rows, D), jnp.float32)
    for shard_index in range(N_MP):
        lower = shard_index * shard_width
        partial_sum = jnp.dot(activated[:, lower:lower + shard_width], out_weight[:, lower:lower + shard_width].T, preferred_element_type=jnp.float32)
        rounded = lax.optimization_barrier(partial_sum.astype(jnp.bfloat16))
        branch = branch + rounded.astype(jnp.float32)
    output = (hidden_wide + branch).astype(jnp.bfloat16)
    grad_scale = 1.0 / math.sqrt(all_rows)
    grad_activated = jnp.dot(cotangent, out_weight, preferred_element_type=jnp.float32)
    sigmoid_value = jax.nn.sigmoid(convolved)
    grad_convolved = grad_activated * sigmoid_value * (1.0 + convolved * (1.0 - sigmoid_value))
    grad_hidden = (cotangent.astype(jnp.float32) + depth_conv(grad_convolved, taps, packed_labels, -1)).astype(jnp.bfloat16)
    out_weight_gradient = grad_scale * jnp.dot(cotangent.T, activated, preferred_element_type=jnp.float32)
    depth_gradient = grad_scale * tap_sums(grad_convolved, hidden_wide, packed_labels)
    in_weight_gradient = grad_scale * jnp.dot(packed.T, grad_hidden, preferred_element_type=jnp.float32)
    return (output, in_weight_gradient, depth_gradient, out_weight_gradient)
```

```python
import math

import jax
import jax.numpy as jnp
from jax import lax
from jax.sharding import PartitionSpec as P

KERNEL = 31
ROWS = 256


def depth_conv(values, weights, labels, direction):
    center = (KERNEL - 1) // 2
    length = values.shape[0]
    padded = jnp.pad(values, ((center, center), (0, 0)))
    padded_labels = jnp.pad(labels, (center, center), constant_values=-1)
    result = jnp.zeros(values.shape, jnp.float32)
    for tap_index in range(KERNEL):
        start = center + direction * (tap_index - center)
        matches = (padded_labels[start : start + length] == labels)[:, None]
        taken = weights[tap_index][None, :] * padded[start : start + length]
        result = result + jnp.where(matches, taken, jnp.zeros_like(taken))
    return result


def tap_sums(grads, values, labels):
    center = (KERNEL - 1) // 2
    length = values.shape[0]
    padded = jnp.pad(values, ((center, center), (0, 0)))
    padded_labels = jnp.pad(labels, (center, center), constant_values=-1)
    rows_list = []
    for tap_index in range(KERNEL):
        matches = (padded_labels[tap_index : tap_index + length] == labels)[:, None]
        taken = grads * padded[tap_index : tap_index + length]
        rows_list.append(jnp.sum(jnp.where(matches, taken, jnp.zeros_like(taken)), axis=0))
    return jnp.stack(rows_list, 0)


def per_device(
    frames, lengths, destinations, offsets, in_weight, depth_weight, out_weight, cotangent
):
    dp_count = lax.axis_size("dp")
    src_rows = frames.shape[0]
    features = frames.shape[1]
    slot_rows = src_rows // dp_count
    entries = lengths.shape[1]
    lengths_row = lengths[0]
    end_rows = jnp.cumsum(lengths_row, dtype=jnp.int32)
    begins = end_rows - lengths_row
    row_ids = jnp.arange(src_rows, dtype=jnp.int32)
    owner_table = (begins[None, :] <= row_ids[:, None]) & (row_ids[:, None] < end_rows[None, :])
    occupied_rows = jnp.any(owner_table, axis=1)
    onehot = owner_table.astype(jnp.int32)

    def lookup(table):
        return jnp.sum(onehot * table[None, :], axis=1, dtype=jnp.int32)

    owner_index = lookup(jnp.arange(entries, dtype=jnp.int32))
    target = lookup(offsets[0]) + row_ids - lookup(begins)
    dest_row = lookup(destinations[0])
    source = lax.axis_index("dp")
    row_label = source * entries + owner_index
    dump_index = dp_count * slot_rows
    slot_index = jnp.where(occupied_rows, dest_row * slot_rows + row_ids % slot_rows, dump_index)
    send_frames = (
        jnp.zeros((dump_index + 1, features), frames.dtype)
        .at[slot_index]
        .set(frames)[:dump_index]
        .reshape(dp_count, slot_rows, features)
    )
    send_target = (
        jnp.full((dump_index + 1,), ROWS, jnp.int32)
        .at[slot_index]
        .set(target)[:dump_index]
        .reshape(dp_count, slot_rows)
    )
    send_label = (
        jnp.full((dump_index + 1,), -1, jnp.int32)
        .at[slot_index]
        .set(row_label)[:dump_index]
        .reshape(dp_count, slot_rows)
    )
    got_frames, got_target, got_label = (
        lax.all_to_all(send_frames, "dp", split_axis=0, concat_axis=0, tiled=True),
        lax.all_to_all(send_target, "dp", split_axis=0, concat_axis=0, tiled=True),
        lax.all_to_all(send_label, "dp", split_axis=0, concat_axis=0, tiled=True),
    )
    flat_target = got_target.reshape(-1)
    packed = (
        jnp.zeros((ROWS + 1, features), frames.dtype)
        .at[flat_target]
        .set(got_frames.reshape(-1, features))[:ROWS]
    )
    packed_labels = (
        jnp.full((ROWS + 1,), -1, jnp.int32).at[flat_target].set(got_label.reshape(-1))[:ROWS]
    )
    hidden = jnp.dot(packed, in_weight, preferred_element_type=jnp.float32).astype(jnp.bfloat16)
    hidden_wide = hidden.astype(jnp.float32)
    taps = depth_weight.astype(jnp.float32)
    convolved = depth_conv(hidden_wide, taps, packed_labels, 1)
    activated = jax.nn.silu(convolved).astype(jnp.bfloat16)
    partial_sum = lax.dot_general(
        activated, out_weight, (((1,), (1,)), ((), ())), preferred_element_type=jnp.float32
    )
    branch = lax.psum_scatter(
        partial_sum.astype(jnp.bfloat16), "mp", scatter_dimension=1, tiled=True
    ).astype(jnp.float32)
    output = (hidden_wide + branch).astype(jnp.bfloat16)
    mp_count = lax.axis_size("mp")
    width = out_weight.shape[1]
    cotangent_blocks = lax.all_gather(cotangent, "mp", axis=0)
    weight_blocks = out_weight.reshape(mp_count, width, width)
    grad_scale = 1.0 / math.sqrt(dp_count * ROWS)
    grad_activated = jnp.einsum(
        "mtc,mci->ti", cotangent_blocks, weight_blocks, preferred_element_type=jnp.float32
    )
    sigmoid_value = jax.nn.sigmoid(convolved)
    grad_convolved = grad_activated * sigmoid_value * (1.0 + convolved * (1.0 - sigmoid_value))
    grad_hidden = (
        cotangent.astype(jnp.float32) + depth_conv(grad_convolved, taps, packed_labels, -1)
    ).astype(jnp.bfloat16)
    term_out = grad_scale * jnp.einsum(
        "mtc,ti->mci", cotangent_blocks, activated, preferred_element_type=jnp.float32
    )
    term_in = grad_scale * lax.dot_general(
        packed, grad_hidden, (((0,), (0,)), ((), ())), preferred_element_type=jnp.float32
    )
    term_depth = grad_scale * tap_sums(grad_convolved, hidden_wide, packed_labels)
    out_rows = term_out.shape[0] * term_out.shape[1] // dp_count
    small = jnp.concatenate((term_in, term_depth), axis=0)
    small_rows = -(-small.shape[0] // dp_count)
    small = jnp.pad(small, ((0, small_rows * dp_count - small.shape[0]), (0, 0)))
    combined = jnp.concatenate(
        (
            term_out.reshape(dp_count, out_rows, width),
            small.reshape(dp_count, small_rows, width),
        ),
        axis=1,
    )
    reduced = lax.psum_scatter(combined, "dp", scatter_dimension=0, tiled=True)[0]
    out_weight_gradient = reduced[:out_rows]
    small_full = lax.all_gather(reduced[out_rows:], "dp", axis=0, tiled=True)
    in_rows = term_in.shape[0]
    in_weight_gradient = small_full[:in_rows]
    depth_gradient = small_full[in_rows : in_rows + term_depth.shape[0]]
    return (output, in_weight_gradient, depth_gradient, out_weight_gradient)


def solution(mesh):
    placed = (
        P("dp", None),
        P("dp", None),
        P("dp", None),
        P("dp", None),
        P(None, "mp"),
        P(None, "mp"),
        P(None, "mp"),
        P("dp", "mp"),
    )
    return jax.shard_map(
        per_device,
        mesh=mesh,
        in_specs=placed,
        out_specs=(P("dp", "mp"), P(None, "mp"), P(None, "mp"), P("dp", "mp")),
        check_vma=False,
    )
```

```python
import math

import jax
import jax.numpy as jnp
from jax import lax
from jax.sharding import PartitionSpec as P

KERNEL = 31
ROWS = 256
DP = ("y", "z", "core")


def depth_conv(values, weights, labels, direction):
    center = (KERNEL - 1) // 2
    length = values.shape[0]
    padded = jnp.pad(values, ((center, center), (0, 0)))
    padded_labels = jnp.pad(labels, (center, center), constant_values=-1)
    result = jnp.zeros(values.shape, jnp.float32)
    for tap_index in range(KERNEL):
        start = center + direction * (tap_index - center)
        matches = (padded_labels[start : start + length] == labels)[:, None]
        taken = weights[tap_index][None, :] * padded[start : start + length]
        result = result + jnp.where(matches, taken, jnp.zeros_like(taken))
    return result


def tap_sums(grads, values, labels):
    center = (KERNEL - 1) // 2
    length = values.shape[0]
    padded = jnp.pad(values, ((center, center), (0, 0)))
    padded_labels = jnp.pad(labels, (center, center), constant_values=-1)
    rows_list = []
    for tap_index in range(KERNEL):
        matches = (padded_labels[tap_index : tap_index + length] == labels)[:, None]
        taken = grads * padded[tap_index : tap_index + length]
        rows_list.append(jnp.sum(jnp.where(matches, taken, jnp.zeros_like(taken)), axis=0))
    return jnp.stack(rows_list, 0)


def per_device(
    frames, lengths, destinations, offsets, in_weight, depth_weight, out_weight, cotangent
):
    dp_count = lax.axis_size(DP)
    src_rows = frames.shape[0]
    features = frames.shape[1]
    slot_rows = src_rows // dp_count
    entries = lengths.shape[1]
    lengths_row = lengths[0]
    end_rows = jnp.cumsum(lengths_row, dtype=jnp.int32)
    begins = end_rows - lengths_row
    row_ids = jnp.arange(src_rows, dtype=jnp.int32)
    owner_table = (begins[None, :] <= row_ids[:, None]) & (row_ids[:, None] < end_rows[None, :])
    occupied_rows = jnp.any(owner_table, axis=1)
    onehot = owner_table.astype(jnp.int32)

    def lookup(table):
        return jnp.sum(onehot * table[None, :], axis=1, dtype=jnp.int32)

    owner_index = lookup(jnp.arange(entries, dtype=jnp.int32))
    target = lookup(offsets[0]) + row_ids - lookup(begins)
    dest_row = lookup(destinations[0])
    source = lax.axis_index(DP)
    row_label = source * entries + owner_index
    dump_index = dp_count * slot_rows
    slot_index = jnp.where(occupied_rows, dest_row * slot_rows + row_ids % slot_rows, dump_index)
    send_frames = (
        jnp.zeros((dump_index + 1, features), frames.dtype)
        .at[slot_index]
        .set(frames)[:dump_index]
        .reshape(dp_count, slot_rows, features)
    )
    send_target = (
        jnp.full((dump_index + 1,), ROWS, jnp.int32)
        .at[slot_index]
        .set(target)[:dump_index]
        .reshape(dp_count, slot_rows)
    )
    send_label = (
        jnp.full((dump_index + 1,), -1, jnp.int32)
        .at[slot_index]
        .set(row_label)[:dump_index]
        .reshape(dp_count, slot_rows)
    )
    got_frames, got_target, got_label = (
        lax.all_to_all(send_frames, DP, split_axis=0, concat_axis=0, tiled=True),
        lax.all_to_all(send_target, DP, split_axis=0, concat_axis=0, tiled=True),
        lax.all_to_all(send_label, DP, split_axis=0, concat_axis=0, tiled=True),
    )
    flat_target = got_target.reshape(-1)
    packed = (
        jnp.zeros((ROWS + 1, features), frames.dtype)
        .at[flat_target]
        .set(got_frames.reshape(-1, features))[:ROWS]
    )
    packed_labels = (
        jnp.full((ROWS + 1,), -1, jnp.int32).at[flat_target].set(got_label.reshape(-1))[:ROWS]
    )
    hidden = jnp.dot(packed, in_weight, preferred_element_type=jnp.float32).astype(jnp.bfloat16)
    hidden_wide = hidden.astype(jnp.float32)
    taps = depth_weight.astype(jnp.float32)
    convolved = depth_conv(hidden_wide, taps, packed_labels, 1)
    activated = jax.nn.silu(convolved).astype(jnp.bfloat16)
    partial_sum = lax.dot_general(
        activated, out_weight, (((1,), (1,)), ((), ())), preferred_element_type=jnp.float32
    )
    branch = lax.psum_scatter(
        partial_sum.astype(jnp.bfloat16), "mp", scatter_dimension=1, tiled=True
    ).astype(jnp.float32)
    output = (hidden_wide + branch).astype(jnp.bfloat16)
    mp_count = lax.axis_size("mp")
    width = out_weight.shape[1]
    cotangent_blocks = lax.all_gather(cotangent, "mp", axis=0)
    weight_blocks = out_weight.reshape(mp_count, width, width)
    grad_scale = 1.0 / math.sqrt(dp_count * ROWS)
    grad_activated = jnp.einsum(
        "mtc,mci->ti", cotangent_blocks, weight_blocks, preferred_element_type=jnp.float32
    )
    sigmoid_value = jax.nn.sigmoid(convolved)
    grad_convolved = grad_activated * sigmoid_value * (1.0 + convolved * (1.0 - sigmoid_value))
    grad_hidden = (
        cotangent.astype(jnp.float32) + depth_conv(grad_convolved, taps, packed_labels, -1)
    ).astype(jnp.bfloat16)
    term_out = grad_scale * jnp.einsum(
        "mtc,ti->mci", cotangent_blocks, activated, preferred_element_type=jnp.float32
    )
    term_in = grad_scale * lax.dot_general(
        packed, grad_hidden, (((0,), (0,)), ((), ())), preferred_element_type=jnp.float32
    )
    term_depth = grad_scale * tap_sums(grad_convolved, hidden_wide, packed_labels)
    out_rows = term_out.shape[0] * term_out.shape[1] // dp_count
    small = jnp.concatenate((term_in, term_depth), axis=0)
    small_rows = -(-small.shape[0] // dp_count)
    small = jnp.pad(small, ((0, small_rows * dp_count - small.shape[0]), (0, 0)))
    combined = jnp.concatenate(
        (
            term_out.reshape(dp_count, out_rows, width),
            small.reshape(dp_count, small_rows, width),
        ),
        axis=1,
    )
    sizes = tuple(lax.axis_size(name) for name in DP)
    staged = combined.reshape(sizes + combined.shape[1:])
    for position in reversed(range(len(DP))):
        staged = lax.psum_scatter(staged, DP[position], scatter_dimension=position, tiled=True)
    reduced = staged.reshape(combined.shape[1:])
    out_weight_gradient = reduced[:out_rows]
    gathered = reduced[out_rows:]
    for position in range(len(DP)):
        gathered = lax.all_gather(gathered, DP[position], axis=position)
    small_full = gathered.reshape(dp_count * small_rows, width)
    in_rows = term_in.shape[0]
    in_weight_gradient = small_full[:in_rows]
    depth_gradient = small_full[in_rows : in_rows + term_depth.shape[0]]
    return (output, in_weight_gradient, depth_gradient, out_weight_gradient)


def split_mesh(mesh):
    devices = mesh.devices
    column = devices[:, 0]
    ys = len({device.coords[1] for device in column})
    zs = len({device.coords[2] for device in column})
    cores = devices.shape[0] // (ys * zs)
    return jax.sharding.Mesh(devices.reshape(ys, zs, cores, devices.shape[1]), DP + ("mp",))


def solution(mesh):
    placed = (
        P(DP, None),
        P(DP, None),
        P(DP, None),
        P(DP, None),
        P(None, "mp"),
        P(None, "mp"),
        P(None, "mp"),
        P(DP, "mp"),
    )
    return jax.shard_map(
        per_device,
        mesh=split_mesh(mesh),
        in_specs=placed,
        out_specs=(P(DP, "mp"), P(None, "mp"), P(None, "mp"), P(DP, "mp")),
        check_vma=False,
    )
```

```python
import math

import jax
import jax.numpy as jnp
from jax import lax
from jax.sharding import PartitionSpec as P

KERNEL = 31
ROWS = 256
DP = ("y", "z", "core")


def depth_conv(values, weights, labels, direction):
    center = (KERNEL - 1) // 2
    length = values.shape[0]
    padded = jnp.pad(values, ((center, center), (0, 0)))
    padded_labels = jnp.pad(labels, (center, center), constant_values=-1)
    result = jnp.zeros(values.shape, jnp.float32)
    for tap_index in range(KERNEL):
        start = center + direction * (tap_index - center)
        matches = (padded_labels[start : start + length] == labels)[:, None]
        taken = weights[tap_index][None, :] * padded[start : start + length]
        result = result + jnp.where(matches, taken, jnp.zeros_like(taken))
    return result


def tap_sums(grads, values, labels):
    center = (KERNEL - 1) // 2
    length = values.shape[0]
    padded = jnp.pad(values, ((center, center), (0, 0)))
    padded_labels = jnp.pad(labels, (center, center), constant_values=-1)
    rows_list = []
    for tap_index in range(KERNEL):
        matches = (padded_labels[tap_index : tap_index + length] == labels)[:, None]
        taken = grads * padded[tap_index : tap_index + length]
        rows_list.append(jnp.sum(jnp.where(matches, taken, jnp.zeros_like(taken)), axis=0))
    return jnp.stack(rows_list, 0)


def per_device(
    frames, lengths, destinations, offsets, in_weight, depth_weight, out_weight, cotangent
):
    dp_count = lax.axis_size(DP)
    src_rows = frames.shape[0]
    features = frames.shape[1]
    slot_rows = src_rows // dp_count
    entries = lengths.shape[1]
    lengths_row = lengths[0]
    end_rows = jnp.cumsum(lengths_row, dtype=jnp.int32)
    begins = end_rows - lengths_row
    row_ids = jnp.arange(src_rows, dtype=jnp.int32)
    owner_table = (begins[None, :] <= row_ids[:, None]) & (row_ids[:, None] < end_rows[None, :])
    occupied_rows = jnp.any(owner_table, axis=1)
    onehot = owner_table.astype(jnp.int32)

    def lookup(table):
        return jnp.sum(onehot * table[None, :], axis=1, dtype=jnp.int32)

    owner_index = lookup(jnp.arange(entries, dtype=jnp.int32))
    target = lookup(offsets[0]) + row_ids - lookup(begins)
    dest_row = lookup(destinations[0])
    source = lax.axis_index(DP)
    row_label = source * entries + owner_index
    dump_index = dp_count * slot_rows
    slot_index = jnp.where(occupied_rows, dest_row * slot_rows + row_ids % slot_rows, dump_index)
    send_frames = (
        jnp.zeros((dump_index + 1, features), frames.dtype)
        .at[slot_index]
        .set(frames)[:dump_index]
        .reshape(dp_count, slot_rows, features)
    )
    send_target = (
        jnp.full((dump_index + 1,), ROWS, jnp.int32)
        .at[slot_index]
        .set(target)[:dump_index]
        .reshape(dp_count, slot_rows)
    )
    send_label = (
        jnp.full((dump_index + 1,), -1, jnp.int32)
        .at[slot_index]
        .set(row_label)[:dump_index]
        .reshape(dp_count, slot_rows)
    )
    got_frames, got_target, got_label = (
        lax.all_to_all(send_frames, DP, split_axis=0, concat_axis=0, tiled=True),
        lax.all_to_all(send_target, DP, split_axis=0, concat_axis=0, tiled=True),
        lax.all_to_all(send_label, DP, split_axis=0, concat_axis=0, tiled=True),
    )
    flat_target = got_target.reshape(-1)
    packed = (
        jnp.zeros((ROWS + 1, features), frames.dtype)
        .at[flat_target]
        .set(got_frames.reshape(-1, features))[:ROWS]
    )
    packed_labels = (
        jnp.full((ROWS + 1,), -1, jnp.int32).at[flat_target].set(got_label.reshape(-1))[:ROWS]
    )
    hidden = jnp.dot(packed, in_weight, preferred_element_type=jnp.float32).astype(jnp.bfloat16)
    hidden_wide = hidden.astype(jnp.float32)
    taps = depth_weight.astype(jnp.float32)
    convolved = depth_conv(hidden_wide, taps, packed_labels, 1)
    activated = jax.nn.silu(convolved).astype(jnp.bfloat16)
    partial_sum = lax.dot_general(
        activated, out_weight, (((1,), (1,)), ((), ())), preferred_element_type=jnp.float32
    )
    branch = lax.psum_scatter(
        partial_sum.astype(jnp.bfloat16), "mp", scatter_dimension=1, tiled=True
    ).astype(jnp.float32)
    output = (hidden_wide + branch).astype(jnp.bfloat16)
    mp_count = lax.axis_size("mp")
    width = out_weight.shape[1]
    cotangent_blocks = lax.all_gather(cotangent, "mp", axis=0)
    weight_blocks = out_weight.reshape(mp_count, width, width)
    grad_scale = 1.0 / math.sqrt(dp_count * ROWS)
    grad_activated = jnp.einsum(
        "mtc,mci->ti", cotangent_blocks, weight_blocks, preferred_element_type=jnp.float32
    )
    sigmoid_value = jax.nn.sigmoid(convolved)
    grad_convolved = grad_activated * sigmoid_value * (1.0 + convolved * (1.0 - sigmoid_value))
    grad_hidden = (
        cotangent.astype(jnp.float32) + depth_conv(grad_convolved, taps, packed_labels, -1)
    ).astype(jnp.bfloat16)
    term_out = grad_scale * jnp.einsum(
        "mtc,ti->mci", cotangent_blocks, activated, preferred_element_type=jnp.float32
    )
    term_in = grad_scale * lax.dot_general(
        packed, grad_hidden, (((0,), (0,)), ((), ())), preferred_element_type=jnp.float32
    )
    term_depth = grad_scale * tap_sums(grad_convolved, hidden_wide, packed_labels)
    out_rows = term_out.shape[0] * term_out.shape[1] // dp_count
    small = jnp.concatenate((term_in, term_depth), axis=0)
    small_rows = -(-small.shape[0] // dp_count)
    small = jnp.pad(small, ((0, small_rows * dp_count - small.shape[0]), (0, 0)))
    combined = jnp.concatenate(
        (
            term_out.reshape(dp_count, out_rows, width),
            small.reshape(dp_count, small_rows, width),
        ),
        axis=1,
    )
    exchanged = lax.all_to_all(combined, DP, split_axis=0, concat_axis=0, tiled=True)
    reduced = jnp.sum(exchanged, axis=0)
    out_weight_gradient = reduced[:out_rows]
    spread = jnp.broadcast_to(reduced[out_rows:][None], (dp_count, small_rows, width))
    gathered = lax.all_to_all(spread, DP, split_axis=0, concat_axis=0, tiled=True)
    small_full = gathered.reshape(dp_count * small_rows, width)
    in_rows = term_in.shape[0]
    in_weight_gradient = small_full[:in_rows]
    depth_gradient = small_full[in_rows : in_rows + term_depth.shape[0]]
    return (output, in_weight_gradient, depth_gradient, out_weight_gradient)


def split_mesh(mesh):
    devices = mesh.devices
    column = devices[:, 0]
    ys = len({device.coords[1] for device in column})
    zs = len({device.coords[2] for device in column})
    cores = devices.shape[0] // (ys * zs)
    return jax.sharding.Mesh(devices.reshape(ys, zs, cores, devices.shape[1]), DP + ("mp",))


def solution(mesh):
    placed = (
        P(DP, None),
        P(DP, None),
        P(DP, None),
        P(DP, None),
        P(None, "mp"),
        P(None, "mp"),
        P(None, "mp"),
        P(DP, "mp"),
    )
    return jax.shard_map(
        per_device,
        mesh=split_mesh(mesh),
        in_specs=placed,
        out_specs=(P(DP, "mp"), P(None, "mp"), P(None, "mp"), P(DP, "mp")),
        check_vma=False,
    )
```

```python
import math

import jax
import jax.numpy as jnp
from jax import lax
from jax.sharding import PartitionSpec as P

KERNEL = 31
ROWS = 256
DP = ("y", "z", "core")


def depth_conv(values, weights, labels, direction):
    center = (KERNEL - 1) // 2
    length = values.shape[0]
    padded = jnp.pad(values, ((center, center), (0, 0)))
    padded_labels = jnp.pad(labels, (center, center), constant_values=-1)
    result = jnp.zeros(values.shape, jnp.float32)
    for tap_index in range(KERNEL):
        start = center + direction * (tap_index - center)
        matches = (padded_labels[start : start + length] == labels)[:, None]
        taken = weights[tap_index][None, :] * padded[start : start + length]
        result = result + jnp.where(matches, taken, jnp.zeros_like(taken))
    return result


def tap_sums(grads, values, labels):
    center = (KERNEL - 1) // 2
    length = values.shape[0]
    padded = jnp.pad(values, ((center, center), (0, 0)))
    padded_labels = jnp.pad(labels, (center, center), constant_values=-1)
    rows_list = []
    for tap_index in range(KERNEL):
        matches = (padded_labels[tap_index : tap_index + length] == labels)[:, None]
        taken = grads * padded[tap_index : tap_index + length]
        rows_list.append(jnp.sum(jnp.where(matches, taken, jnp.zeros_like(taken)), axis=0))
    return jnp.stack(rows_list, 0)


def per_device(
    frames, lengths, destinations, offsets, in_weight, depth_weight, out_weight, cotangent
):
    dp_count = lax.axis_size(DP)
    src_rows = frames.shape[0]
    features = frames.shape[1]
    slot_rows = src_rows // dp_count
    entries = lengths.shape[1]
    lengths_row = lengths[0]
    end_rows = jnp.cumsum(lengths_row, dtype=jnp.int32)
    begins = end_rows - lengths_row
    row_ids = jnp.arange(src_rows, dtype=jnp.int32)
    owner_index = jnp.sum((end_rows[None, :] <= row_ids[:, None]).astype(jnp.int32), axis=1)
    occupied_rows = owner_index < entries
    owner = jnp.minimum(owner_index, entries - 1)
    target = jnp.where(occupied_rows, offsets[0][owner] + row_ids - begins[owner], ROWS)
    block_ids = jnp.arange(dp_count, dtype=jnp.int32)
    block_dest = jnp.where(occupied_rows[::slot_rows], destinations[0][owner[::slot_rows]], -1)
    chosen = block_dest[None, :] == block_ids[:, None]
    block_of = jnp.sum(jnp.where(chosen, block_ids[None, :], 0), axis=1)
    has_block = jnp.any(chosen, axis=1)
    codes = jnp.stack((target, owner), axis=1).astype(frames.dtype)
    blocks = jnp.concatenate((frames, codes), axis=1).reshape(dp_count, slot_rows, features + 2)
    send = jnp.take(blocks, block_of, axis=0)
    send = send.at[:, :, features].set(
        jnp.where(has_block[:, None], send[:, :, features], jnp.asarray(ROWS, frames.dtype))
    )
    got = lax.all_to_all(send, DP, split_axis=0, concat_axis=0, tiled=True)
    got = got.reshape(dp_count * slot_rows, features + 2)
    got_target = got[:, features].astype(jnp.int32)
    got_label = (row_ids // slot_rows) * entries + got[:, features + 1].astype(jnp.int32)
    place = got_target[None, :] == jnp.arange(ROWS, dtype=jnp.int32)[:, None]
    packed = jnp.dot(
        place.astype(frames.dtype), got[:, :features], preferred_element_type=jnp.float32
    ).astype(frames.dtype)
    packed_labels = jnp.max(jnp.where(place, got_label[None, :], -1), axis=1)
    hidden = jnp.dot(packed, in_weight, preferred_element_type=jnp.float32).astype(jnp.bfloat16)
    hidden_wide = hidden.astype(jnp.float32)
    taps = depth_weight.astype(jnp.float32)
    convolved = depth_conv(hidden_wide, taps, packed_labels, 1)
    activated = jax.nn.silu(convolved).astype(jnp.bfloat16)
    partial_sum = lax.dot_general(
        activated, out_weight, (((1,), (1,)), ((), ())), preferred_element_type=jnp.float32
    )
    branch = lax.psum_scatter(
        partial_sum.astype(jnp.bfloat16), "mp", scatter_dimension=1, tiled=True
    ).astype(jnp.float32)
    output = (hidden_wide + branch).astype(jnp.bfloat16)
    mp_count = lax.axis_size("mp")
    width = out_weight.shape[1]
    cotangent_blocks = lax.all_gather(cotangent, "mp", axis=0)
    weight_blocks = out_weight.reshape(mp_count, width, width)
    grad_scale = 1.0 / math.sqrt(dp_count * ROWS)
    grad_activated = jnp.einsum(
        "mtc,mci->ti", cotangent_blocks, weight_blocks, preferred_element_type=jnp.float32
    )
    sigmoid_value = jax.nn.sigmoid(convolved)
    grad_convolved = grad_activated * sigmoid_value * (1.0 + convolved * (1.0 - sigmoid_value))
    grad_hidden = (
        cotangent.astype(jnp.float32) + depth_conv(grad_convolved, taps, packed_labels, -1)
    ).astype(jnp.bfloat16)
    term_out = grad_scale * jnp.einsum(
        "mtc,ti->mci", cotangent_blocks, activated, preferred_element_type=jnp.float32
    )
    term_in = grad_scale * lax.dot_general(
        packed, grad_hidden, (((0,), (0,)), ((), ())), preferred_element_type=jnp.float32
    )
    term_depth = grad_scale * tap_sums(grad_convolved, hidden_wide, packed_labels)
    out_rows = term_out.shape[0] * term_out.shape[1] // dp_count
    small = jnp.concatenate((term_in, term_depth), axis=0)
    small_rows = -(-small.shape[0] // dp_count)
    small = jnp.pad(small, ((0, small_rows * dp_count - small.shape[0]), (0, 0)))
    combined = jnp.concatenate(
        (
            term_out.reshape(dp_count, out_rows, width),
            small.reshape(dp_count, small_rows, width),
        ),
        axis=1,
    )
    exchanged = lax.all_to_all(combined, DP, split_axis=0, concat_axis=0, tiled=True)
    reduced = jnp.sum(exchanged, axis=0)
    out_weight_gradient = reduced[:out_rows]
    spread = jnp.broadcast_to(
        reduced[out_rows:].astype(jnp.bfloat16)[None], (dp_count, small_rows, width)
    )
    gathered = lax.all_to_all(spread, DP, split_axis=0, concat_axis=0, tiled=True)
    small_full = gathered.reshape(dp_count * small_rows, width).astype(jnp.float32)
    in_rows = term_in.shape[0]
    in_weight_gradient = small_full[:in_rows]
    depth_gradient = small_full[in_rows : in_rows + term_depth.shape[0]]
    return (output, in_weight_gradient, depth_gradient, out_weight_gradient)


def split_mesh(mesh):
    devices = mesh.devices
    column = devices[:, 0]
    ys = len({device.coords[1] for device in column})
    zs = len({device.coords[2] for device in column})
    cores = devices.shape[0] // (ys * zs)
    return jax.sharding.Mesh(devices.reshape(ys, zs, cores, devices.shape[1]), DP + ("mp",))


def solution(mesh):
    placed = (
        P(DP, None),
        P(DP, None),
        P(DP, None),
        P(DP, None),
        P(None, "mp"),
        P(None, "mp"),
        P(None, "mp"),
        P(DP, "mp"),
    )
    return jax.shard_map(
        per_device,
        mesh=split_mesh(mesh),
        in_specs=placed,
        out_specs=(P(DP, "mp"), P(None, "mp"), P(None, "mp"), P(DP, "mp")),
        check_vma=False,
    )
```

```python
import math

import jax
import jax.numpy as jnp
from jax import lax
from jax.sharding import PartitionSpec as P

KERNEL = 31
ROWS = 256
DP = ("y", "z", "core")


def depth_conv(values, weights, labels, direction):
    center = (KERNEL - 1) // 2
    length = values.shape[0]
    padded = jnp.pad(values, ((center, center), (0, 0)))
    padded_labels = jnp.pad(labels, (center, center), constant_values=-1)
    result = jnp.zeros(values.shape, jnp.float32)
    for tap_index in range(KERNEL):
        start = center + direction * (tap_index - center)
        matches = (padded_labels[start : start + length] == labels)[:, None]
        taken = weights[tap_index][None, :] * padded[start : start + length]
        result = result + jnp.where(matches, taken, jnp.zeros_like(taken))
    return result


def tap_sums(grads, values, labels):
    center = (KERNEL - 1) // 2
    length = values.shape[0]
    padded = jnp.pad(values, ((center, center), (0, 0)))
    padded_labels = jnp.pad(labels, (center, center), constant_values=-1)
    rows_list = []
    for tap_index in range(KERNEL):
        matches = (padded_labels[tap_index : tap_index + length] == labels)[:, None]
        taken = grads * padded[tap_index : tap_index + length]
        rows_list.append(jnp.sum(jnp.where(matches, taken, jnp.zeros_like(taken)), axis=0))
    return jnp.stack(rows_list, 0)


def per_device(
    frames, lengths, destinations, offsets, in_weight, depth_weight, out_weight, cotangent
):
    dp_count = lax.axis_size(DP)
    src_rows = frames.shape[0]
    features = frames.shape[1]
    slot_rows = src_rows // dp_count
    entries = lengths.shape[1]
    lengths_row = lengths[0]
    end_rows = jnp.cumsum(lengths_row, dtype=jnp.int32)
    begins = end_rows - lengths_row
    row_ids = jnp.arange(src_rows, dtype=jnp.int32)
    owner_table = (begins[None, :] <= row_ids[:, None]) & (row_ids[:, None] < end_rows[None, :])
    occupied_rows = jnp.any(owner_table, axis=1)

    def lookup(table):
        return jnp.sum(jnp.where(owner_table, table[None, :], 0), axis=1, dtype=jnp.int32)

    entry_ids = jnp.arange(entries, dtype=jnp.int32)
    owner = lookup(entry_ids)
    target = lookup(offsets[0] - begins) + row_ids + 1
    block_ids = jnp.arange(dp_count, dtype=jnp.int32)
    block_dest = jnp.where(occupied_rows, lookup(destinations[0]), -1)[::slot_rows]
    chosen = (block_dest[None, :] == block_ids[:, None]).astype(frames.dtype)
    codes = jnp.stack((jnp.where(occupied_rows, target, 0), owner), axis=1).astype(frames.dtype)
    blocks = jnp.concatenate((frames, codes), axis=1).reshape(dp_count, slot_rows, features + 2)
    send = jnp.einsum(
        "dk,krf->drf", chosen, blocks, preferred_element_type=jnp.float32
    ).astype(frames.dtype)
    got = lax.all_to_all(send, DP, split_axis=0, concat_axis=0, tiled=True)
    got = got.reshape(dp_count * slot_rows, features + 2)
    got_target = got[:, features].astype(jnp.int32) - 1
    got_label = (row_ids // slot_rows) * entries + got[:, features + 1].astype(jnp.int32)
    place = got_target[None, :] == jnp.arange(ROWS, dtype=jnp.int32)[:, None]
    packed = jnp.dot(
        place.astype(frames.dtype), got[:, :features], preferred_element_type=jnp.float32
    ).astype(frames.dtype)
    packed_labels = jnp.max(jnp.where(place, got_label[None, :], -1), axis=1)
    hidden = jnp.dot(packed, in_weight, preferred_element_type=jnp.float32).astype(jnp.bfloat16)
    hidden_wide = hidden.astype(jnp.float32)
    taps = depth_weight.astype(jnp.float32)
    convolved = depth_conv(hidden_wide, taps, packed_labels, 1)
    activated = jax.nn.silu(convolved).astype(jnp.bfloat16)
    partial_sum = lax.dot_general(
        activated, out_weight, (((1,), (1,)), ((), ())), preferred_element_type=jnp.float32
    )
    branch = lax.psum_scatter(
        partial_sum.astype(jnp.bfloat16), "mp", scatter_dimension=1, tiled=True
    ).astype(jnp.float32)
    output = (hidden_wide + branch).astype(jnp.bfloat16)
    mp_count = lax.axis_size("mp")
    width = out_weight.shape[1]
    cotangent_blocks = lax.all_gather(cotangent, "mp", axis=0)
    weight_blocks = out_weight.reshape(mp_count, width, width)
    grad_scale = 1.0 / math.sqrt(dp_count * ROWS)
    grad_activated = jnp.einsum(
        "mtc,mci->ti", cotangent_blocks, weight_blocks, preferred_element_type=jnp.float32
    )
    sigmoid_value = jax.nn.sigmoid(convolved)
    grad_convolved = grad_activated * sigmoid_value * (1.0 + convolved * (1.0 - sigmoid_value))
    grad_hidden = (
        cotangent.astype(jnp.float32) + depth_conv(grad_convolved, taps, packed_labels, -1)
    ).astype(jnp.bfloat16)
    term_out = grad_scale * jnp.einsum(
        "mtc,ti->mci", cotangent_blocks, activated, preferred_element_type=jnp.float32
    )
    term_in = grad_scale * lax.dot_general(
        packed, grad_hidden, (((0,), (0,)), ((), ())), preferred_element_type=jnp.float32
    )
    term_depth = grad_scale * tap_sums(grad_convolved, hidden_wide, packed_labels)
    out_rows = term_out.shape[0] * term_out.shape[1] // dp_count
    small = jnp.concatenate((term_in, term_depth), axis=0)
    small_rows = -(-small.shape[0] // dp_count)
    small = jnp.pad(small, ((0, small_rows * dp_count - small.shape[0]), (0, 0)))
    combined = jnp.concatenate(
        (
            term_out.reshape(dp_count, out_rows, width),
            small.reshape(dp_count, small_rows, width),
        ),
        axis=1,
    )
    core = lax.axis_index(DP[-1])
    cores = lax.axis_size(DP[-1])
    paired = combined.reshape((dp_count // cores, cores) + combined.shape[1:])
    keep = jnp.where(core == 0, paired[:, 0], paired[:, 1])
    give = jnp.where(core == 0, paired[:, 1], paired[:, 0])
    pair_sum = keep + lax.ppermute(give, DP[-1], [(0, 1), (1, 0)])
    exchanged = lax.all_to_all(pair_sum, DP[:-1], split_axis=0, concat_axis=0, tiled=True)
    reduced = jnp.sum(exchanged, axis=0)
    out_weight_gradient = reduced[:out_rows]
    spread = jnp.broadcast_to(
        reduced[out_rows:].astype(jnp.bfloat16)[None], (dp_count, small_rows, width)
    )
    gathered = lax.all_to_all(spread, DP, split_axis=0, concat_axis=0, tiled=True)
    small_full = gathered.reshape(dp_count * small_rows, width).astype(jnp.float32)
    in_rows = term_in.shape[0]
    in_weight_gradient = small_full[:in_rows]
    depth_gradient = small_full[in_rows : in_rows + term_depth.shape[0]]
    return (output, in_weight_gradient, depth_gradient, out_weight_gradient)


def split_mesh(mesh):
    devices = mesh.devices
    column = devices[:, 0]
    ys = len({device.coords[1] for device in column})
    zs = len({device.coords[2] for device in column})
    cores = devices.shape[0] // (ys * zs)
    return jax.sharding.Mesh(devices.reshape(ys, zs, cores, devices.shape[1]), DP + ("mp",))


def solution(mesh):
    placed = (
        P(DP, None),
        P(DP, None),
        P(DP, None),
        P(DP, None),
        P(None, "mp"),
        P(None, "mp"),
        P(None, "mp"),
        P(DP, "mp"),
    )
    return jax.shard_map(
        per_device,
        mesh=split_mesh(mesh),
        in_specs=placed,
        out_specs=(P(DP, "mp"), P(None, "mp"), P(None, "mp"), P(DP, "mp")),
        check_vma=False,
    )
```

```python
import math

import jax
import jax.numpy as jnp
from jax import lax
from jax.sharding import PartitionSpec as P

KERNEL = 31
ROWS = 256
DP = ("y", "z", "core")


def depth_conv(values, weights, labels, direction):
    center = (KERNEL - 1) // 2
    length = values.shape[0]
    padded = jnp.pad(values, ((center, center), (0, 0)))
    padded_labels = jnp.pad(labels, (center, center), constant_values=-1)
    result = jnp.zeros(values.shape, jnp.float32)
    for tap_index in range(KERNEL):
        start = center + direction * (tap_index - center)
        matches = (padded_labels[start : start + length] == labels)[:, None]
        taken = weights[tap_index][None, :] * padded[start : start + length]
        result = result + jnp.where(matches, taken, jnp.zeros_like(taken))
    return result


def tap_sums(grads, values, labels):
    center = (KERNEL - 1) // 2
    length = values.shape[0]
    padded = jnp.pad(values, ((center, center), (0, 0)))
    padded_labels = jnp.pad(labels, (center, center), constant_values=-1)
    rows_list = []
    for tap_index in range(KERNEL):
        matches = (padded_labels[tap_index : tap_index + length] == labels)[:, None]
        taken = grads * padded[tap_index : tap_index + length]
        rows_list.append(jnp.sum(jnp.where(matches, taken, jnp.zeros_like(taken)), axis=0))
    return jnp.stack(rows_list, 0)


def per_device(
    frames, lengths, destinations, offsets, in_weight, depth_weight, out_weight, cotangent
):
    dp_count = lax.axis_size(DP)
    src_rows = frames.shape[0]
    features = frames.shape[1]
    slot_rows = src_rows // dp_count
    entries = lengths.shape[1]
    lengths_row = lengths[0]
    end_rows = jnp.cumsum(lengths_row, dtype=jnp.int32)
    begins = end_rows - lengths_row
    row_ids = jnp.arange(src_rows, dtype=jnp.int32)
    owner_table = (begins[None, :] <= row_ids[:, None]) & (row_ids[:, None] < end_rows[None, :])
    occupied_rows = jnp.any(owner_table, axis=1)

    def lookup(table):
        return jnp.sum(jnp.where(owner_table, table[None, :], 0), axis=1, dtype=jnp.int32)

    entry_ids = jnp.arange(entries, dtype=jnp.int32)
    owner = lookup(entry_ids)
    target = lookup(offsets[0] - begins) + row_ids + 1
    block_ids = jnp.arange(dp_count, dtype=jnp.int32)
    block_dest = jnp.where(occupied_rows, lookup(destinations[0]), -1)[::slot_rows]
    chosen = (block_dest[None, :] == block_ids[:, None]).astype(frames.dtype)
    codes = jnp.stack((jnp.where(occupied_rows, target, 0), owner), axis=1).astype(frames.dtype)
    blocks = jnp.concatenate((frames, codes), axis=1).reshape(dp_count, slot_rows, features + 2)
    send = jnp.einsum(
        "dk,krf->drf", chosen, blocks, preferred_element_type=jnp.float32
    ).astype(frames.dtype)
    got = lax.all_to_all(send, DP, split_axis=0, concat_axis=0, tiled=True)
    got = got.reshape(dp_count * slot_rows, features + 2)
    got_target = got[:, features].astype(jnp.int32) - 1
    got_label = (row_ids // slot_rows) * entries + got[:, features + 1].astype(jnp.int32)
    place = got_target[None, :] == jnp.arange(ROWS, dtype=jnp.int32)[:, None]
    packed = jnp.dot(
        place.astype(frames.dtype), got[:, :features], preferred_element_type=jnp.float32
    ).astype(frames.dtype)
    packed_labels = jnp.max(jnp.where(place, got_label[None, :], -1), axis=1)
    hidden = jnp.dot(packed, in_weight, preferred_element_type=jnp.float32).astype(jnp.bfloat16)
    hidden_wide = hidden.astype(jnp.float32)
    taps = depth_weight.astype(jnp.float32)
    convolved = depth_conv(hidden_wide, taps, packed_labels, 1)
    activated = jax.nn.silu(convolved).astype(jnp.bfloat16)
    partial_sum = lax.dot_general(
        activated, out_weight, (((1,), (1,)), ((), ())), preferred_element_type=jnp.float32
    )
    mp_count = lax.axis_size("mp")
    width = out_weight.shape[1]
    block_sums = partial_sum.astype(jnp.bfloat16).reshape(ROWS, mp_count, width)
    branch_parts = lax.all_to_all(
        jnp.swapaxes(block_sums, 0, 1), "mp", split_axis=0, concat_axis=0, tiled=True
    )
    branch = jnp.sum(branch_parts.astype(jnp.float32), axis=0)
    output = (hidden_wide + branch).astype(jnp.bfloat16)
    model_index = lax.axis_index("mp")
    shifted = [cotangent] + [
        lax.ppermute(cotangent, "mp", [(m, (m + k) % mp_count) for m in range(mp_count)])
        for k in range(1, mp_count)
    ]
    order = (model_index - jnp.arange(mp_count, dtype=jnp.int32)) % mp_count
    cotangent_blocks = jnp.take(jnp.stack(shifted, axis=0), order, axis=0)
    weight_blocks = out_weight.reshape(mp_count, width, width)
    grad_scale = 1.0 / math.sqrt(dp_count * ROWS)
    grad_activated = jnp.einsum(
        "mtc,mci->ti", cotangent_blocks, weight_blocks, preferred_element_type=jnp.float32
    )
    sigmoid_value = jax.nn.sigmoid(convolved)
    grad_convolved = grad_activated * sigmoid_value * (1.0 + convolved * (1.0 - sigmoid_value))
    grad_hidden = (
        cotangent.astype(jnp.float32) + depth_conv(grad_convolved, taps, packed_labels, -1)
    ).astype(jnp.bfloat16)
    term_out = grad_scale * jnp.einsum(
        "mtc,ti->mci", cotangent_blocks, activated, preferred_element_type=jnp.float32
    )
    term_in = grad_scale * lax.dot_general(
        packed, grad_hidden, (((0,), (0,)), ((), ())), preferred_element_type=jnp.float32
    )
    term_depth = grad_scale * tap_sums(grad_convolved, hidden_wide, packed_labels)
    out_rows = term_out.shape[0] * term_out.shape[1] // dp_count
    small = jnp.concatenate((term_in, term_depth), axis=0)
    small_rows = -(-small.shape[0] // dp_count)
    small = jnp.pad(small, ((0, small_rows * dp_count - small.shape[0]), (0, 0)))
    combined = jnp.concatenate(
        (
            term_out.reshape(dp_count, out_rows, width),
            small.reshape(dp_count, small_rows, width),
        ),
        axis=1,
    )
    core = lax.axis_index(DP[-1])
    cores = lax.axis_size(DP[-1])
    paired = combined.reshape((dp_count // cores, cores) + combined.shape[1:])
    keep = jnp.where(core == 0, paired[:, 0], paired[:, 1])
    give = jnp.where(core == 0, paired[:, 1], paired[:, 0])
    pair_sum = keep + lax.ppermute(give, DP[-1], [(0, 1), (1, 0)])
    exchanged = lax.all_to_all(pair_sum, DP[:-1], split_axis=0, concat_axis=0, tiled=True)
    reduced = jnp.sum(exchanged, axis=0)
    out_weight_gradient = reduced[:out_rows]
    spread = jnp.broadcast_to(
        reduced[out_rows:].astype(jnp.bfloat16)[None], (dp_count, small_rows, width)
    )
    gathered = lax.all_to_all(spread, DP, split_axis=0, concat_axis=0, tiled=True)
    small_full = gathered.reshape(dp_count * small_rows, width).astype(jnp.float32)
    in_rows = term_in.shape[0]
    in_weight_gradient = small_full[:in_rows]
    depth_gradient = small_full[in_rows : in_rows + term_depth.shape[0]]
    return (output, in_weight_gradient, depth_gradient, out_weight_gradient)


def split_mesh(mesh):
    devices = mesh.devices
    column = devices[:, 0]
    ys = len({device.coords[1] for device in column})
    zs = len({device.coords[2] for device in column})
    cores = devices.shape[0] // (ys * zs)
    return jax.sharding.Mesh(devices.reshape(ys, zs, cores, devices.shape[1]), DP + ("mp",))


def solution(mesh):
    placed = (
        P(DP, None),
        P(DP, None),
        P(DP, None),
        P(DP, None),
        P(None, "mp"),
        P(None, "mp"),
        P(None, "mp"),
        P(DP, "mp"),
    )
    return jax.shard_map(
        per_device,
        mesh=split_mesh(mesh),
        in_specs=placed,
        out_specs=(P(DP, "mp"), P(None, "mp"), P(None, "mp"), P(DP, "mp")),
        check_vma=False,
    )
```

```python
import math

import jax
import jax.numpy as jnp
from jax import lax
from jax.sharding import PartitionSpec as P

KERNEL = 31
ROWS = 256
DP = ("y", "z", "core")


def depth_conv(values, weights, labels, direction):
    center = (KERNEL - 1) // 2
    length = values.shape[0]
    padded = jnp.pad(values, ((center, center), (0, 0)))
    padded_labels = jnp.pad(labels, (center, center), constant_values=-1)
    result = jnp.zeros(values.shape, jnp.float32)
    for tap_index in range(KERNEL):
        start = center + direction * (tap_index - center)
        matches = (padded_labels[start : start + length] == labels)[:, None]
        taken = weights[tap_index][None, :] * padded[start : start + length]
        result = result + jnp.where(matches, taken, jnp.zeros_like(taken))
    return result


def tap_sums(grads, values, labels):
    center = (KERNEL - 1) // 2
    length = values.shape[0]
    padded = jnp.pad(values, ((center, center), (0, 0)))
    padded_labels = jnp.pad(labels, (center, center), constant_values=-1)
    rows_list = []
    for tap_index in range(KERNEL):
        matches = (padded_labels[tap_index : tap_index + length] == labels)[:, None]
        taken = grads * padded[tap_index : tap_index + length]
        rows_list.append(jnp.sum(jnp.where(matches, taken, jnp.zeros_like(taken)), axis=0))
    return jnp.stack(rows_list, 0)


def per_device(
    frames, lengths, destinations, offsets, in_weight, depth_weight, out_weight, cotangent
):
    dp_count = lax.axis_size(DP)
    src_rows = frames.shape[0]
    features = frames.shape[1]
    slot_rows = src_rows // dp_count
    entries = lengths.shape[1]
    lengths_row = lengths[0]
    end_rows = jnp.cumsum(lengths_row, dtype=jnp.int32)
    begins = end_rows - lengths_row
    row_ids = jnp.arange(src_rows, dtype=jnp.int32)
    owner_table = (begins[None, :] <= row_ids[:, None]) & (row_ids[:, None] < end_rows[None, :])
    occupied_rows = jnp.any(owner_table, axis=1)

    def lookup(table):
        return jnp.sum(jnp.where(owner_table, table[None, :], 0), axis=1, dtype=jnp.int32)

    entry_ids = jnp.arange(entries, dtype=jnp.int32)
    owner = lookup(entry_ids)
    target = lookup(offsets[0] - begins) + row_ids + 1
    block_ids = jnp.arange(dp_count, dtype=jnp.int32)
    block_dest = jnp.where(occupied_rows, lookup(destinations[0]), -1)[::slot_rows]
    chosen = (block_dest[None, :] == block_ids[:, None]).astype(frames.dtype)
    codes = jnp.stack((jnp.where(occupied_rows, target, 0), owner), axis=1).astype(frames.dtype)
    blocks = jnp.concatenate((frames, codes), axis=1).reshape(dp_count, slot_rows, features + 2)
    send = jnp.einsum(
        "dk,krf->drf", chosen, blocks, preferred_element_type=jnp.float32
    ).astype(frames.dtype)
    got = lax.all_to_all(send, DP, split_axis=0, concat_axis=0, tiled=True)
    got = got.reshape(dp_count * slot_rows, features + 2)
    got_target = got[:, features].astype(jnp.int32) - 1
    got_label = (row_ids // slot_rows) * entries + got[:, features + 1].astype(jnp.int32)
    place = got_target[None, :] == jnp.arange(ROWS, dtype=jnp.int32)[:, None]
    packed = jnp.dot(
        place.astype(frames.dtype), got[:, :features], preferred_element_type=jnp.float32
    ).astype(frames.dtype)
    packed_labels = jnp.max(jnp.where(place, got_label[None, :], -1), axis=1)
    hidden = jnp.dot(packed, in_weight, preferred_element_type=jnp.float32).astype(jnp.bfloat16)
    hidden_wide = hidden.astype(jnp.float32)
    taps = depth_weight.astype(jnp.float32)
    convolved = depth_conv(hidden_wide, taps, packed_labels, 1)
    activated = jax.nn.silu(convolved).astype(jnp.bfloat16)
    partial_sum = lax.dot_general(
        activated, out_weight, (((1,), (1,)), ((), ())), preferred_element_type=jnp.float32
    )
    mp_count = lax.axis_size("mp")
    width = out_weight.shape[1]
    block_sums = partial_sum.astype(jnp.bfloat16).reshape(ROWS, mp_count, width)
    branch_parts = lax.all_to_all(
        jnp.swapaxes(block_sums, 0, 1), "mp", split_axis=0, concat_axis=0, tiled=True
    )
    branch = jnp.sum(branch_parts.astype(jnp.float32), axis=0)
    output = (hidden_wide + branch).astype(jnp.bfloat16)
    model_index = lax.axis_index("mp")
    shifted = [cotangent] + [
        lax.ppermute(cotangent, "mp", [(m, (m + k) % mp_count) for m in range(mp_count)])
        for k in range(1, mp_count)
    ]
    order = (model_index - jnp.arange(mp_count, dtype=jnp.int32)) % mp_count
    cotangent_blocks = jnp.take(jnp.stack(shifted, axis=0), order, axis=0)
    weight_blocks = out_weight.reshape(mp_count, width, width)
    grad_scale = 1.0 / math.sqrt(dp_count * ROWS)
    grad_activated = jnp.einsum(
        "mtc,mci->ti", cotangent_blocks, weight_blocks, preferred_element_type=jnp.float32
    )
    sigmoid_value = jax.nn.sigmoid(convolved)
    grad_convolved = grad_activated * sigmoid_value * (1.0 + convolved * (1.0 - sigmoid_value))
    grad_hidden = (
        cotangent.astype(jnp.float32) + depth_conv(grad_convolved, taps, packed_labels, -1)
    ).astype(jnp.bfloat16)
    term_out = grad_scale * jnp.einsum(
        "mtc,ti->mci", cotangent_blocks, activated, preferred_element_type=jnp.float32
    )
    term_in = grad_scale * lax.dot_general(
        packed, grad_hidden, (((0,), (0,)), ((), ())), preferred_element_type=jnp.float32
    )
    term_depth = grad_scale * tap_sums(grad_convolved, hidden_wide, packed_labels)
    out_rows = term_out.shape[0] * term_out.shape[1] // dp_count
    small = jnp.concatenate((term_in, term_depth), axis=0)
    small_rows = -(-small.shape[0] // dp_count)
    small = jnp.pad(small, ((0, small_rows * dp_count - small.shape[0]), (0, 0)))
    combined = jnp.concatenate(
        (
            term_out.reshape(dp_count, out_rows, width),
            small.reshape(dp_count, small_rows, width),
        ),
        axis=1,
    )
    steps = []
    for name in DP:
        size = lax.axis_size(name)
        bits = size.bit_length() - 1
        steps += [(name, size, bit) for bit in reversed(range(bits))]
    staged = combined.reshape((2,) * len(steps) + combined.shape[1:])
    for name, size, bit in reversed(steps):
        mine = (lax.axis_index(name) >> bit) & 1
        last = staged.ndim - 3
        keep = lax.dynamic_index_in_dim(staged, mine, last, keepdims=False)
        give = lax.dynamic_index_in_dim(staged, 1 - mine, last, keepdims=False)
        staged = keep + lax.ppermute(give, name, [(i, i ^ (1 << bit)) for i in range(size)])
    reduced = staged
    out_weight_gradient = reduced[:out_rows]
    gathered = reduced[out_rows:].astype(jnp.bfloat16)
    for count, (name, size, bit) in enumerate(steps):
        mine = (lax.axis_index(name) >> bit) & 1
        other = lax.ppermute(gathered, name, [(i, i ^ (1 << bit)) for i in range(size)])
        gathered = jnp.where(
            mine == 0, jnp.stack((gathered, other), count), jnp.stack((other, gathered), count)
        )
    small_full = gathered.reshape(dp_count * small_rows, width).astype(jnp.float32)
    in_rows = term_in.shape[0]
    in_weight_gradient = small_full[:in_rows]
    depth_gradient = small_full[in_rows : in_rows + term_depth.shape[0]]
    return (output, in_weight_gradient, depth_gradient, out_weight_gradient)


def split_mesh(mesh):
    devices = mesh.devices
    column = devices[:, 0]
    ys = len({device.coords[1] for device in column})
    zs = len({device.coords[2] for device in column})
    cores = devices.shape[0] // (ys * zs)
    return jax.sharding.Mesh(devices.reshape(ys, zs, cores, devices.shape[1]), DP + ("mp",))


def solution(mesh):
    placed = (
        P(DP, None),
        P(DP, None),
        P(DP, None),
        P(DP, None),
        P(None, "mp"),
        P(None, "mp"),
        P(None, "mp"),
        P(DP, "mp"),
    )
    return jax.shard_map(
        per_device,
        mesh=split_mesh(mesh),
        in_specs=placed,
        out_specs=(P(DP, "mp"), P(None, "mp"), P(None, "mp"), P(DP, "mp")),
        check_vma=False,
    )
```

```python
import math

import jax
import jax.numpy as jnp
from jax import lax
from jax.sharding import PartitionSpec as P

KERNEL = 31
ROWS = 256
DP = ("y", "z", "core")


def depth_conv(values, weights, labels, direction):
    center = (KERNEL - 1) // 2
    length = values.shape[0]
    padded = jnp.pad(values, ((center, center), (0, 0)))
    padded_labels = jnp.pad(labels, (center, center), constant_values=-1)
    result = jnp.zeros(values.shape, jnp.float32)
    for tap_index in range(KERNEL):
        start = center + direction * (tap_index - center)
        matches = (padded_labels[start : start + length] == labels)[:, None]
        taken = weights[tap_index][None, :] * padded[start : start + length]
        result = result + jnp.where(matches, taken, jnp.zeros_like(taken))
    return result


def tap_sums(grads, values, labels):
    center = (KERNEL - 1) // 2
    length = values.shape[0]
    padded = jnp.pad(values, ((center, center), (0, 0)))
    padded_labels = jnp.pad(labels, (center, center), constant_values=-1)
    rows_list = []
    for tap_index in range(KERNEL):
        matches = (padded_labels[tap_index : tap_index + length] == labels)[:, None]
        taken = grads * padded[tap_index : tap_index + length]
        rows_list.append(jnp.sum(jnp.where(matches, taken, jnp.zeros_like(taken)), axis=0))
    return jnp.stack(rows_list, 0)


def per_device(
    frames, lengths, destinations, offsets, in_weight, depth_weight, out_weight, cotangent
):
    dp_count = lax.axis_size(DP)
    src_rows = frames.shape[0]
    features = frames.shape[1]
    slot_rows = src_rows // dp_count
    entries = lengths.shape[1]
    lengths_row = lengths[0]
    end_rows = jnp.cumsum(lengths_row, dtype=jnp.int32)
    begins = end_rows - lengths_row
    row_ids = jnp.arange(src_rows, dtype=jnp.int32)
    owner_table = (begins[None, :] <= row_ids[:, None]) & (row_ids[:, None] < end_rows[None, :])
    occupied_rows = jnp.any(owner_table, axis=1)

    def lookup(table):
        return jnp.sum(jnp.where(owner_table, table[None, :], 0), axis=1, dtype=jnp.int32)

    entry_ids = jnp.arange(entries, dtype=jnp.int32)
    owner = lookup(entry_ids)
    target = lookup(offsets[0] - begins) + row_ids + 1
    block_ids = jnp.arange(dp_count, dtype=jnp.int32)
    block_dest = jnp.where(occupied_rows, lookup(destinations[0]), -1)[::slot_rows]
    chosen = (block_dest[None, :] == block_ids[:, None]).astype(frames.dtype)
    codes = jnp.stack((jnp.where(occupied_rows, target, 0), owner), axis=1).astype(frames.dtype)
    blocks = jnp.concatenate((frames, codes), axis=1).reshape(dp_count, slot_rows, features + 2)
    send = jnp.einsum(
        "dk,krf->drf", chosen, blocks, preferred_element_type=jnp.float32
    ).astype(frames.dtype)
    got = lax.all_to_all(send, DP, split_axis=0, concat_axis=0, tiled=True)
    got = got.reshape(dp_count * slot_rows, features + 2)
    got_target = got[:, features].astype(jnp.int32) - 1
    got_label = (row_ids // slot_rows) * entries + got[:, features + 1].astype(jnp.int32)
    place = got_target[None, :] == jnp.arange(ROWS, dtype=jnp.int32)[:, None]
    packed = jnp.dot(
        place.astype(frames.dtype), got[:, :features], preferred_element_type=jnp.float32
    ).astype(frames.dtype)
    packed_labels = jnp.max(jnp.where(place, got_label[None, :], -1), axis=1)
    hidden = jnp.dot(packed, in_weight, preferred_element_type=jnp.float32).astype(jnp.bfloat16)
    hidden_wide = hidden.astype(jnp.float32)
    taps = depth_weight.astype(jnp.float32)
    convolved = depth_conv(hidden_wide, taps, packed_labels, 1)
    activated = jax.nn.silu(convolved).astype(jnp.bfloat16)
    partial_sum = lax.dot_general(
        activated, out_weight, (((1,), (1,)), ((), ())), preferred_element_type=jnp.float32
    )
    mp_count = lax.axis_size("mp")
    width = out_weight.shape[1]
    block_sums = partial_sum.astype(jnp.bfloat16).reshape(ROWS, mp_count, width)
    branch_parts = lax.all_to_all(
        jnp.swapaxes(block_sums, 0, 1), "mp", split_axis=0, concat_axis=0, tiled=True
    )
    branch = jnp.sum(branch_parts.astype(jnp.float32), axis=0)
    output = (hidden_wide + branch).astype(jnp.bfloat16)
    model_index = lax.axis_index("mp")
    shifted = [cotangent] + [
        lax.ppermute(cotangent, "mp", [(m, (m + k) % mp_count) for m in range(mp_count)])
        for k in range(1, mp_count)
    ]
    order = (model_index - jnp.arange(mp_count, dtype=jnp.int32)) % mp_count
    cotangent_blocks = jnp.take(jnp.stack(shifted, axis=0), order, axis=0)
    weight_blocks = out_weight.reshape(mp_count, width, width)
    grad_scale = 1.0 / math.sqrt(dp_count * ROWS)
    grad_activated = jnp.einsum(
        "mtc,mci->ti", cotangent_blocks, weight_blocks, preferred_element_type=jnp.float32
    )
    sigmoid_value = jax.nn.sigmoid(convolved)
    grad_convolved = grad_activated * sigmoid_value * (1.0 + convolved * (1.0 - sigmoid_value))
    grad_hidden = (
        cotangent.astype(jnp.float32) + depth_conv(grad_convolved, taps, packed_labels, -1)
    ).astype(jnp.bfloat16)
    term_out = grad_scale * jnp.einsum(
        "mtc,ti->mci", cotangent_blocks, activated, preferred_element_type=jnp.float32
    )
    term_in = grad_scale * lax.dot_general(
        packed, grad_hidden, (((0,), (0,)), ((), ())), preferred_element_type=jnp.float32
    )
    term_depth = grad_scale * tap_sums(grad_convolved, hidden_wide, packed_labels)
    out_rows = term_out.shape[0] * term_out.shape[1] // dp_count
    small = jnp.concatenate((term_in, term_depth), axis=0)
    small_rows = -(-small.shape[0] // dp_count)
    small = jnp.pad(small, ((0, small_rows * dp_count - small.shape[0]), (0, 0)))
    combined = jnp.concatenate(
        (
            term_out.reshape(dp_count, out_rows, width),
            small.reshape(dp_count, small_rows, width),
        ),
        axis=1,
    )
    core = lax.axis_index(DP[-1])
    cores = lax.axis_size(DP[-1])
    paired = combined.reshape((dp_count // cores, cores) + combined.shape[1:])
    keep = jnp.where(core == 0, paired[:, 0], paired[:, 1])
    give = jnp.where(core == 0, paired[:, 1], paired[:, 0])
    pair_sum = keep + lax.ppermute(give, DP[-1], [(0, 1), (1, 0)])
    exchanged = lax.all_to_all(pair_sum, DP[:-1], split_axis=0, concat_axis=0, tiled=True)
    reduced = jnp.sum(exchanged, axis=0)
    out_weight_gradient = reduced[:out_rows]
    spread = jnp.broadcast_to(
        reduced[out_rows:].astype(jnp.bfloat16).reshape(1, small_rows * width),
        (dp_count, small_rows * width),
    )
    gathered = lax.all_to_all(spread, DP, split_axis=0, concat_axis=0, tiled=True)
    small_full = gathered.reshape(dp_count * small_rows, width).astype(jnp.float32)
    in_rows = term_in.shape[0]
    in_weight_gradient = small_full[:in_rows]
    depth_gradient = small_full[in_rows : in_rows + term_depth.shape[0]]
    return (output, in_weight_gradient, depth_gradient, out_weight_gradient)


def split_mesh(mesh):
    devices = mesh.devices
    column = devices[:, 0]
    ys = len({device.coords[1] for device in column})
    zs = len({device.coords[2] for device in column})
    cores = devices.shape[0] // (ys * zs)
    return jax.sharding.Mesh(devices.reshape(ys, zs, cores, devices.shape[1]), DP + ("mp",))


def solution(mesh):
    placed = (
        P(DP, None),
        P(DP, None),
        P(DP, None),
        P(DP, None),
        P(None, "mp"),
        P(None, "mp"),
        P(None, "mp"),
        P(DP, "mp"),
    )
    return jax.shard_map(
        per_device,
        mesh=split_mesh(mesh),
        in_specs=placed,
        out_specs=(P(DP, "mp"), P(None, "mp"), P(None, "mp"), P(DP, "mp")),
        check_vma=False,
    )
```

```python
import math

import jax
import jax.numpy as jnp
from jax import lax
from jax.sharding import PartitionSpec as P

KERNEL = 31
ROWS = 256
DP = ("y", "z", "core")


def depth_conv(values, weights, labels, direction):
    center = (KERNEL - 1) // 2
    length = values.shape[0]
    padded = jnp.pad(values, ((center, center), (0, 0)))
    padded_labels = jnp.pad(labels, (center, center), constant_values=-1)
    result = jnp.zeros(values.shape, jnp.float32)
    for tap_index in range(KERNEL):
        start = center + direction * (tap_index - center)
        matches = (padded_labels[start : start + length] == labels)[:, None]
        taken = weights[tap_index][None, :] * padded[start : start + length]
        result = result + jnp.where(matches, taken, jnp.zeros_like(taken))
    return result


def tap_sums(grads, values, labels):
    center = (KERNEL - 1) // 2
    length = values.shape[0]
    padded = jnp.pad(values, ((center, center), (0, 0)))
    padded_labels = jnp.pad(labels, (center, center), constant_values=-1)
    rows_list = []
    for tap_index in range(KERNEL):
        matches = (padded_labels[tap_index : tap_index + length] == labels)[:, None]
        taken = grads * padded[tap_index : tap_index + length]
        rows_list.append(jnp.sum(jnp.where(matches, taken, jnp.zeros_like(taken)), axis=0))
    return jnp.stack(rows_list, 0)


def per_device(
    frames, lengths, destinations, offsets, in_weight, depth_weight, out_weight, cotangent
):
    dp_count = lax.axis_size(DP)
    src_rows = frames.shape[0]
    features = frames.shape[1]
    slot_rows = src_rows // dp_count
    entries = lengths.shape[1]
    lengths_row = lengths[0]
    end_rows = jnp.cumsum(lengths_row, dtype=jnp.int32)
    begins = end_rows - lengths_row
    row_ids = jnp.arange(src_rows, dtype=jnp.int32)
    owner_table = (begins[None, :] <= row_ids[:, None]) & (row_ids[:, None] < end_rows[None, :])
    occupied_rows = jnp.any(owner_table, axis=1)

    def lookup(table):
        return jnp.sum(jnp.where(owner_table, table[None, :], 0), axis=1, dtype=jnp.int32)

    entry_ids = jnp.arange(entries, dtype=jnp.int32)
    owner = lookup(entry_ids)
    target = lookup(offsets[0] - begins) + row_ids + 1
    block_ids = jnp.arange(dp_count, dtype=jnp.int32)
    block_dest = jnp.where(occupied_rows, lookup(destinations[0]), -1)[::slot_rows]
    chosen = (block_dest[None, :] == block_ids[:, None]).astype(frames.dtype)
    codes = jnp.stack((jnp.where(occupied_rows, target, 0), owner), axis=1).astype(frames.dtype)
    blocks = jnp.concatenate((frames, codes), axis=1).reshape(dp_count, slot_rows, features + 2)
    send = jnp.einsum(
        "dk,krf->drf", chosen, blocks, preferred_element_type=jnp.float32
    ).astype(frames.dtype)
    got = lax.all_to_all(send, DP, split_axis=0, concat_axis=0, tiled=True)
    got = got.reshape(dp_count * slot_rows, features + 2)
    got_target = got[:, features].astype(jnp.int32) - 1
    got_label = (row_ids // slot_rows) * entries + got[:, features + 1].astype(jnp.int32)
    place = got_target[None, :] == jnp.arange(ROWS, dtype=jnp.int32)[:, None]
    packed = jnp.dot(
        place.astype(frames.dtype), got[:, :features], preferred_element_type=jnp.float32
    ).astype(frames.dtype)
    packed_labels = jnp.max(jnp.where(place, got_label[None, :], -1), axis=1)
    hidden = jnp.dot(packed, in_weight, preferred_element_type=jnp.float32).astype(jnp.bfloat16)
    hidden_wide = hidden.astype(jnp.float32)
    taps = depth_weight.astype(jnp.float32)
    convolved = depth_conv(hidden_wide, taps, packed_labels, 1)
    activated = jax.nn.silu(convolved).astype(jnp.bfloat16)
    partial_sum = lax.dot_general(
        activated, out_weight, (((1,), (1,)), ((), ())), preferred_element_type=jnp.float32
    )
    mp_count = lax.axis_size("mp")
    width = out_weight.shape[1]
    block_sums = partial_sum.astype(jnp.bfloat16).reshape(ROWS, mp_count, width)
    branch_parts = lax.all_to_all(
        jnp.swapaxes(block_sums, 0, 1), "mp", split_axis=0, concat_axis=0, tiled=True
    )
    branch = jnp.sum(branch_parts.astype(jnp.float32), axis=0)
    output = (hidden_wide + branch).astype(jnp.bfloat16)
    model_index = lax.axis_index("mp")
    shifted = [cotangent] + [
        lax.ppermute(cotangent, "mp", [(m, (m + k) % mp_count) for m in range(mp_count)])
        for k in range(1, mp_count)
    ]
    order = (model_index - jnp.arange(mp_count, dtype=jnp.int32)) % mp_count
    cotangent_blocks = jnp.take(jnp.stack(shifted, axis=0), order, axis=0)
    weight_blocks = out_weight.reshape(mp_count, width, width)
    grad_scale = 1.0 / math.sqrt(dp_count * ROWS)
    grad_activated = jnp.einsum(
        "mtc,mci->ti", cotangent_blocks, weight_blocks, preferred_element_type=jnp.float32
    )
    sigmoid_value = jax.nn.sigmoid(convolved)
    grad_convolved = grad_activated * sigmoid_value * (1.0 + convolved * (1.0 - sigmoid_value))
    grad_hidden = (
        cotangent.astype(jnp.float32) + depth_conv(grad_convolved, taps, packed_labels, -1)
    ).astype(jnp.bfloat16)
    term_out = grad_scale * jnp.einsum(
        "mtc,ti->mci", cotangent_blocks, activated, preferred_element_type=jnp.float32
    )
    term_in = grad_scale * lax.dot_general(
        packed, grad_hidden, (((0,), (0,)), ((), ())), preferred_element_type=jnp.float32
    )
    term_depth = grad_scale * tap_sums(grad_convolved, hidden_wide, packed_labels)
    out_rows = term_out.shape[0] * term_out.shape[1] // dp_count
    small = jnp.concatenate((term_in, term_depth), axis=0)
    small_rows = -(-small.shape[0] // dp_count)
    small = jnp.pad(small, ((0, small_rows * dp_count - small.shape[0]), (0, 0)))
    combined = jnp.concatenate(
        (
            term_out.reshape(dp_count, out_rows, width),
            small.reshape(dp_count, small_rows, width),
        ),
        axis=1,
    )
    core = lax.axis_index(DP[-1])
    cores = lax.axis_size(DP[-1])
    paired = combined.reshape((dp_count // cores, cores) + combined.shape[1:])
    keep = jnp.where(core == 0, paired[:, 0], paired[:, 1])
    give = jnp.where(core == 0, paired[:, 1], paired[:, 0])
    pair_sum = keep + lax.ppermute(give, DP[-1], [(0, 1), (1, 0)])
    reduced = pair_sum.reshape(
        tuple(lax.axis_size(name) for name in DP[:-1]) + pair_sum.shape[1:]
    )
    for position in reversed(range(len(DP) - 1)):
        reduced = jnp.sum(
            lax.all_to_all(
                reduced, DP[position], split_axis=position, concat_axis=position, tiled=True
            ),
            axis=position,
        )
    out_weight_gradient = reduced[:out_rows]
    spread = jnp.broadcast_to(
        reduced[out_rows:].astype(jnp.bfloat16)[None], (dp_count, small_rows, width)
    )
    gathered = lax.all_to_all(spread, DP, split_axis=0, concat_axis=0, tiled=True)
    small_full = gathered.reshape(dp_count * small_rows, width).astype(jnp.float32)
    in_rows = term_in.shape[0]
    in_weight_gradient = small_full[:in_rows]
    depth_gradient = small_full[in_rows : in_rows + term_depth.shape[0]]
    return (output, in_weight_gradient, depth_gradient, out_weight_gradient)


def split_mesh(mesh):
    devices = mesh.devices
    column = devices[:, 0]
    ys = len({device.coords[1] for device in column})
    zs = len({device.coords[2] for device in column})
    cores = devices.shape[0] // (ys * zs)
    return jax.sharding.Mesh(devices.reshape(ys, zs, cores, devices.shape[1]), DP + ("mp",))


def solution(mesh):
    placed = (
        P(DP, None),
        P(DP, None),
        P(DP, None),
        P(DP, None),
        P(None, "mp"),
        P(None, "mp"),
        P(None, "mp"),
        P(DP, "mp"),
    )
    return jax.shard_map(
        per_device,
        mesh=split_mesh(mesh),
        in_specs=placed,
        out_specs=(P(DP, "mp"), P(None, "mp"), P(None, "mp"), P(DP, "mp")),
        check_vma=False,
    )
```

```python
import math

import jax
import jax.numpy as jnp
from jax import lax
from jax.sharding import PartitionSpec as P

KERNEL = 31
ROWS = 256
DP = ("y", "z", "core")


def depth_conv(values, weights, labels, direction):
    center = (KERNEL - 1) // 2
    length = values.shape[0]
    padded = jnp.pad(values, ((center, center), (0, 0)))
    padded_labels = jnp.pad(labels, (center, center), constant_values=-1)
    result = jnp.zeros(values.shape, jnp.float32)
    for tap_index in range(KERNEL):
        start = center + direction * (tap_index - center)
        matches = (padded_labels[start : start + length] == labels)[:, None]
        taken = weights[tap_index][None, :] * padded[start : start + length]
        result = result + jnp.where(matches, taken, jnp.zeros_like(taken))
    return result


def tap_sums(grads, values, labels):
    center = (KERNEL - 1) // 2
    length = values.shape[0]
    padded = jnp.pad(values, ((center, center), (0, 0)))
    padded_labels = jnp.pad(labels, (center, center), constant_values=-1)
    rows_list = []
    for tap_index in range(KERNEL):
        matches = (padded_labels[tap_index : tap_index + length] == labels)[:, None]
        taken = grads * padded[tap_index : tap_index + length]
        rows_list.append(jnp.sum(jnp.where(matches, taken, jnp.zeros_like(taken)), axis=0))
    return jnp.stack(rows_list, 0)


def per_device(
    frames, lengths, destinations, offsets, in_weight, depth_weight, out_weight, cotangent
):
    dp_count = lax.axis_size(DP)
    src_rows = frames.shape[0]
    features = frames.shape[1]
    slot_rows = src_rows // dp_count
    entries = lengths.shape[1]
    lengths_row = lengths[0]
    end_rows = jnp.cumsum(lengths_row, dtype=jnp.int32)
    begins = end_rows - lengths_row
    row_ids = jnp.arange(src_rows, dtype=jnp.int32)
    owner_table = (begins[None, :] <= row_ids[:, None]) & (row_ids[:, None] < end_rows[None, :])
    occupied_rows = jnp.any(owner_table, axis=1)

    def lookup(table):
        return jnp.sum(jnp.where(owner_table, table[None, :], 0), axis=1, dtype=jnp.int32)

    entry_ids = jnp.arange(entries, dtype=jnp.int32)
    owner = lookup(entry_ids)
    target = lookup(offsets[0] - begins) + row_ids + 1
    block_ids = jnp.arange(dp_count, dtype=jnp.int32)
    block_dest = jnp.where(occupied_rows, lookup(destinations[0]), -1)[::slot_rows]
    chosen = (block_dest[None, :] == block_ids[:, None]).astype(frames.dtype)
    codes = jnp.stack((jnp.where(occupied_rows, target, 0), owner), axis=1).astype(frames.dtype)
    lanes = -(-(features + 2) // 128) * 128
    filler = jnp.zeros((src_rows, lanes - features - 2), frames.dtype)
    blocks = jnp.concatenate((frames, codes, filler), axis=1).reshape(dp_count, slot_rows * lanes)
    send = jnp.dot(chosen, blocks, preferred_element_type=jnp.float32).astype(frames.dtype)
    got = lax.all_to_all(
        send.reshape(dp_count, slot_rows, lanes), DP, split_axis=0, concat_axis=0, tiled=True
    )
    got = got.reshape(dp_count * slot_rows, lanes)
    got_target = got[:, features].astype(jnp.int32) - 1
    got_label = (row_ids // slot_rows) * entries + got[:, features + 1].astype(jnp.int32)
    place = got_target[None, :] == jnp.arange(ROWS, dtype=jnp.int32)[:, None]
    packed = jnp.dot(
        place.astype(frames.dtype), got[:, :features], preferred_element_type=jnp.float32
    ).astype(frames.dtype)
    packed_labels = jnp.max(jnp.where(place, got_label[None, :], -1), axis=1)
    hidden = jnp.dot(packed, in_weight, preferred_element_type=jnp.float32).astype(jnp.bfloat16)
    hidden_wide = hidden.astype(jnp.float32)
    taps = depth_weight.astype(jnp.float32)
    convolved = depth_conv(hidden_wide, taps, packed_labels, 1)
    activated = jax.nn.silu(convolved).astype(jnp.bfloat16)
    partial_sum = lax.dot_general(
        activated, out_weight, (((1,), (1,)), ((), ())), preferred_element_type=jnp.float32
    )
    mp_count = lax.axis_size("mp")
    width = out_weight.shape[1]
    block_sums = partial_sum.astype(jnp.bfloat16).reshape(ROWS, mp_count, width)
    branch_parts = lax.all_to_all(
        jnp.swapaxes(block_sums, 0, 1), "mp", split_axis=0, concat_axis=0, tiled=True
    )
    branch = jnp.sum(branch_parts.astype(jnp.float32), axis=0)
    output = (hidden_wide + branch).astype(jnp.bfloat16)
    model_index = lax.axis_index("mp")
    shifted = [cotangent] + [
        lax.ppermute(cotangent, "mp", [(m, (m + k) % mp_count) for m in range(mp_count)])
        for k in range(1, mp_count)
    ]
    order = (model_index - jnp.arange(mp_count, dtype=jnp.int32)) % mp_count
    cotangent_blocks = jnp.take(jnp.stack(shifted, axis=0), order, axis=0)
    weight_blocks = out_weight.reshape(mp_count, width, width)
    grad_scale = 1.0 / math.sqrt(dp_count * ROWS)
    grad_activated = jnp.einsum(
        "mtc,mci->ti", cotangent_blocks, weight_blocks, preferred_element_type=jnp.float32
    )
    sigmoid_value = jax.nn.sigmoid(convolved)
    grad_convolved = grad_activated * sigmoid_value * (1.0 + convolved * (1.0 - sigmoid_value))
    grad_hidden = (
        cotangent.astype(jnp.float32) + depth_conv(grad_convolved, taps, packed_labels, -1)
    ).astype(jnp.bfloat16)
    term_out = grad_scale * jnp.einsum(
        "mtc,ti->mci", cotangent_blocks, activated, preferred_element_type=jnp.float32
    )
    term_in = grad_scale * lax.dot_general(
        packed, grad_hidden, (((0,), (0,)), ((), ())), preferred_element_type=jnp.float32
    )
    term_depth = grad_scale * tap_sums(grad_convolved, hidden_wide, packed_labels)
    out_rows = term_out.shape[0] * term_out.shape[1] // dp_count
    small = jnp.concatenate((term_in, term_depth), axis=0)
    small_rows = -(-small.shape[0] // dp_count)
    small = jnp.pad(small, ((0, small_rows * dp_count - small.shape[0]), (0, 0)))
    core = lax.axis_index(DP[-1])
    cores = lax.axis_size(DP[-1])
    paired_out = term_out.reshape(dp_count // cores, cores, out_rows, width)
    paired_small = small.reshape(dp_count // cores, cores, small_rows, width)

    def halves(side):
        return jnp.concatenate(
            (
                lax.dynamic_index_in_dim(paired_out, side, 1, keepdims=False),
                lax.dynamic_index_in_dim(paired_small, side, 1, keepdims=False),
            ),
            axis=1,
        )

    keep = halves(core)
    give = halves(1 - core)
    pair_sum = keep + lax.ppermute(give, DP[-1], [(0, 1), (1, 0)])
    exchanged = lax.all_to_all(pair_sum, DP[:-1], split_axis=0, concat_axis=0, tiled=True)
    reduced = jnp.sum(exchanged, axis=0)
    out_weight_gradient = reduced[:out_rows]
    spread = jnp.broadcast_to(
        reduced[out_rows:].astype(jnp.bfloat16)[None], (dp_count, small_rows, width)
    )
    gathered = lax.all_to_all(spread, DP, split_axis=0, concat_axis=0, tiled=True)
    small_full = gathered.reshape(dp_count * small_rows, width).astype(jnp.float32)
    in_rows = term_in.shape[0]
    in_weight_gradient = small_full[:in_rows]
    depth_gradient = small_full[in_rows : in_rows + term_depth.shape[0]]
    return (output, in_weight_gradient, depth_gradient, out_weight_gradient)


def split_mesh(mesh):
    devices = mesh.devices
    column = devices[:, 0]
    ys = len({device.coords[1] for device in column})
    zs = len({device.coords[2] for device in column})
    cores = devices.shape[0] // (ys * zs)
    return jax.sharding.Mesh(devices.reshape(ys, zs, cores, devices.shape[1]), DP + ("mp",))


def solution(mesh):
    placed = (
        P(DP, None),
        P(DP, None),
        P(DP, None),
        P(DP, None),
        P(None, "mp"),
        P(None, "mp"),
        P(None, "mp"),
        P(DP, "mp"),
    )
    return jax.shard_map(
        per_device,
        mesh=split_mesh(mesh),
        in_specs=placed,
        out_specs=(P(DP, "mp"), P(None, "mp"), P(None, "mp"), P(DP, "mp")),
        check_vma=False,
    )
```

```python
import math

import jax
import jax.numpy as jnp
from jax import lax
from jax.sharding import PartitionSpec as P

KERNEL = 31
ROWS = 256
DP = ("y", "z", "core")


def depth_conv(values, weights, labels, direction):
    center = (KERNEL - 1) // 2
    length = values.shape[0]
    padded = jnp.pad(values, ((center, center), (0, 0)))
    padded_labels = jnp.pad(labels, (center, center), constant_values=-1)
    result = jnp.zeros(values.shape, jnp.float32)
    for tap_index in range(KERNEL):
        start = center + direction * (tap_index - center)
        matches = (padded_labels[start : start + length] == labels)[:, None]
        taken = weights[tap_index][None, :] * padded[start : start + length]
        result = result + jnp.where(matches, taken, jnp.zeros_like(taken))
    return result


def tap_sums(grads, values, labels):
    center = (KERNEL - 1) // 2
    length = values.shape[0]
    padded = jnp.pad(values, ((center, center), (0, 0)))
    padded_labels = jnp.pad(labels, (center, center), constant_values=-1)
    rows_list = []
    for tap_index in range(KERNEL):
        matches = (padded_labels[tap_index : tap_index + length] == labels)[:, None]
        taken = grads * padded[tap_index : tap_index + length]
        rows_list.append(jnp.sum(jnp.where(matches, taken, jnp.zeros_like(taken)), axis=0))
    return jnp.stack(rows_list, 0)


def per_device(
    frames, lengths, destinations, offsets, in_weight, depth_weight, out_weight, cotangent
):
    dp_count = lax.axis_size(DP)
    src_rows = frames.shape[0]
    features = frames.shape[1]
    slot_rows = src_rows // dp_count
    entries = lengths.shape[1]
    lengths_row = lengths[0]
    end_rows = jnp.cumsum(lengths_row, dtype=jnp.int32)
    begins = end_rows - lengths_row
    row_ids = jnp.arange(src_rows, dtype=jnp.int32)
    owner_table = (begins[None, :] <= row_ids[:, None]) & (row_ids[:, None] < end_rows[None, :])
    occupied_rows = jnp.any(owner_table, axis=1)

    def lookup(table):
        return jnp.sum(jnp.where(owner_table, table[None, :], 0), axis=1, dtype=jnp.int32)

    entry_ids = jnp.arange(entries, dtype=jnp.int32)
    owner = lookup(entry_ids)
    target = lookup(offsets[0] - begins) + row_ids + 1
    block_ids = jnp.arange(dp_count, dtype=jnp.int32)
    block_dest = jnp.where(occupied_rows, lookup(destinations[0]), -1)[::slot_rows]
    chosen = (block_dest[None, :] == block_ids[:, None]).astype(frames.dtype)
    codes = jnp.stack((jnp.where(occupied_rows, target, 0), owner), axis=1).astype(frames.dtype)
    blocks = jnp.concatenate((frames, codes), axis=1).reshape(dp_count, slot_rows, features + 2)
    send = jnp.einsum(
        "dk,krf->drf", chosen, blocks, preferred_element_type=jnp.float32
    ).astype(frames.dtype)
    got = lax.all_to_all(send, DP, split_axis=0, concat_axis=0, tiled=True)
    got = got.reshape(dp_count * slot_rows, features + 2)
    got_target = got[:, features].astype(jnp.int32) - 1
    got_label = (row_ids // slot_rows) * entries + got[:, features + 1].astype(jnp.int32)
    place = got_target[None, :] == jnp.arange(ROWS, dtype=jnp.int32)[:, None]
    packed = jnp.dot(
        place.astype(frames.dtype), got[:, :features], preferred_element_type=jnp.float32
    ).astype(frames.dtype)
    packed_labels = jnp.max(jnp.where(place, got_label[None, :], -1), axis=1)
    hidden = jnp.dot(packed, in_weight, preferred_element_type=jnp.float32).astype(jnp.bfloat16)
    hidden_wide = hidden.astype(jnp.float32)
    taps = depth_weight.astype(jnp.float32)
    convolved = depth_conv(hidden_wide, taps, packed_labels, 1)
    activated = jax.nn.silu(convolved).astype(jnp.bfloat16)
    partial_sum = lax.dot_general(
        activated, out_weight, (((1,), (1,)), ((), ())), preferred_element_type=jnp.float32
    )
    mp_count = lax.axis_size("mp")
    width = out_weight.shape[1]
    block_sums = partial_sum.astype(jnp.bfloat16).reshape(ROWS, mp_count, width)
    branch_parts = lax.all_to_all(
        jnp.swapaxes(block_sums, 0, 1), "mp", split_axis=0, concat_axis=0, tiled=True
    )
    branch = jnp.sum(branch_parts.astype(jnp.float32), axis=0)
    output = (hidden_wide + branch).astype(jnp.bfloat16)
    model_index = lax.axis_index("mp")
    shifted = [cotangent] + [
        lax.ppermute(cotangent, "mp", [(m, (m + k) % mp_count) for m in range(mp_count)])
        for k in range(1, mp_count)
    ]
    order = (model_index - jnp.arange(mp_count, dtype=jnp.int32)) % mp_count
    cotangent_blocks = jnp.take(jnp.stack(shifted, axis=0), order, axis=0)
    weight_blocks = out_weight.reshape(mp_count, width, width)
    grad_scale = 1.0 / math.sqrt(dp_count * ROWS)
    core = lax.axis_index(DP[-1])
    cores = lax.axis_size(DP[-1])

    def reduce_scatter(part):
        paired = part.reshape((dp_count // cores, cores) + part.shape[1:])
        keep = jnp.where(core == 0, paired[:, 0], paired[:, 1])
        give = jnp.where(core == 0, paired[:, 1], paired[:, 0])
        pair_sum = keep + lax.ppermute(give, DP[-1], [(0, 1), (1, 0)])
        exchanged = lax.all_to_all(pair_sum, DP[:-1], split_axis=0, concat_axis=0, tiled=True)
        return jnp.sum(exchanged, axis=0)

    term_out = grad_scale * jnp.einsum(
        "mtc,ti->mci", cotangent_blocks, activated, preferred_element_type=jnp.float32
    )
    out_rows = term_out.shape[0] * term_out.shape[1] // dp_count
    out_weight_gradient = reduce_scatter(term_out.reshape(dp_count, out_rows, width))
    grad_activated = jnp.einsum(
        "mtc,mci->ti", cotangent_blocks, weight_blocks, preferred_element_type=jnp.float32
    )
    sigmoid_value = jax.nn.sigmoid(convolved)
    grad_convolved = grad_activated * sigmoid_value * (1.0 + convolved * (1.0 - sigmoid_value))
    grad_hidden = (
        cotangent.astype(jnp.float32) + depth_conv(grad_convolved, taps, packed_labels, -1)
    ).astype(jnp.bfloat16)
    term_in = grad_scale * lax.dot_general(
        packed, grad_hidden, (((0,), (0,)), ((), ())), preferred_element_type=jnp.float32
    )
    term_depth = grad_scale * tap_sums(grad_convolved, hidden_wide, packed_labels)
    out_weight_gradient, term_in, term_depth = lax.optimization_barrier(
        (out_weight_gradient, term_in, term_depth)
    )
    small = jnp.concatenate((term_in, term_depth), axis=0)
    small_rows = -(-small.shape[0] // dp_count)
    small = jnp.pad(small, ((0, small_rows * dp_count - small.shape[0]), (0, 0)))
    small_part = reduce_scatter(small.reshape(dp_count, small_rows, width))
    spread = jnp.broadcast_to(
        small_part.astype(jnp.bfloat16)[None], (dp_count, small_rows, width)
    )
    gathered = lax.all_to_all(spread, DP, split_axis=0, concat_axis=0, tiled=True)
    small_full = gathered.reshape(dp_count * small_rows, width).astype(jnp.float32)
    in_rows = term_in.shape[0]
    in_weight_gradient = small_full[:in_rows]
    depth_gradient = small_full[in_rows : in_rows + term_depth.shape[0]]
    return (output, in_weight_gradient, depth_gradient, out_weight_gradient)


def split_mesh(mesh):
    devices = mesh.devices
    column = devices[:, 0]
    ys = len({device.coords[1] for device in column})
    zs = len({device.coords[2] for device in column})
    cores = devices.shape[0] // (ys * zs)
    return jax.sharding.Mesh(devices.reshape(ys, zs, cores, devices.shape[1]), DP + ("mp",))


def solution(mesh):
    placed = (
        P(DP, None),
        P(DP, None),
        P(DP, None),
        P(DP, None),
        P(None, "mp"),
        P(None, "mp"),
        P(None, "mp"),
        P(DP, "mp"),
    )
    return jax.shard_map(
        per_device,
        mesh=split_mesh(mesh),
        in_specs=placed,
        out_specs=(P(DP, "mp"), P(None, "mp"), P(None, "mp"), P(DP, "mp")),
        check_vma=False,
    )
```

```python
import math

import jax
import jax.numpy as jnp
from jax import lax
from jax.sharding import PartitionSpec as P

KERNEL = 31
ROWS = 256
DP = ("y", "z", "core")


def depth_conv(values, weights, labels, direction):
    center = (KERNEL - 1) // 2
    length = values.shape[0]
    padded = jnp.pad(values, ((center, center), (0, 0)))
    padded_labels = jnp.pad(labels, (center, center), constant_values=-1)
    result = jnp.zeros(values.shape, jnp.float32)
    for tap_index in range(KERNEL):
        start = center + direction * (tap_index - center)
        matches = (padded_labels[start : start + length] == labels)[:, None]
        taken = weights[tap_index][None, :] * padded[start : start + length]
        result = result + jnp.where(matches, taken, jnp.zeros_like(taken))
    return result


def tap_sums(grads, values, labels):
    center = (KERNEL - 1) // 2
    length = values.shape[0]
    padded = jnp.pad(values, ((center, center), (0, 0)))
    padded_labels = jnp.pad(labels, (center, center), constant_values=-1)
    rows_list = []
    for tap_index in range(KERNEL):
        matches = (padded_labels[tap_index : tap_index + length] == labels)[:, None]
        taken = grads * padded[tap_index : tap_index + length]
        rows_list.append(jnp.sum(jnp.where(matches, taken, jnp.zeros_like(taken)), axis=0))
    return jnp.stack(rows_list, 0)


def per_device(
    frames, lengths, destinations, offsets, in_weight, depth_weight, out_weight, cotangent
):
    dp_count = lax.axis_size(DP)
    src_rows = frames.shape[0]
    features = frames.shape[1]
    slot_rows = src_rows // dp_count
    entries = lengths.shape[1]
    lengths_row = lengths[0]
    end_rows = jnp.cumsum(lengths_row, dtype=jnp.int32)
    begins = end_rows - lengths_row
    row_ids = jnp.arange(src_rows, dtype=jnp.int32)
    owner_table = (begins[None, :] <= row_ids[:, None]) & (row_ids[:, None] < end_rows[None, :])
    occupied_rows = jnp.any(owner_table, axis=1)

    def lookup(table):
        return jnp.sum(jnp.where(owner_table, table[None, :], 0), axis=1, dtype=jnp.int32)

    entry_ids = jnp.arange(entries, dtype=jnp.int32)
    owner = lookup(entry_ids)
    target = lookup(offsets[0] - begins) + row_ids + 1
    block_ids = jnp.arange(dp_count, dtype=jnp.int32)
    block_dest = jnp.where(occupied_rows, lookup(destinations[0]), -1)[::slot_rows]
    chosen = (block_dest[None, :] == block_ids[:, None]).astype(frames.dtype)
    codes = jnp.stack((jnp.where(occupied_rows, target, 0), owner), axis=1).astype(frames.dtype)
    blocks = jnp.concatenate((frames, codes), axis=1).reshape(dp_count, slot_rows, features + 2)
    send = jnp.einsum(
        "dk,krf->drf", chosen, blocks, preferred_element_type=jnp.float32
    ).astype(frames.dtype)
    got = lax.all_to_all(send, DP, split_axis=0, concat_axis=0, tiled=True)
    got = got.reshape(dp_count * slot_rows, features + 2)
    got_target = got[:, features].astype(jnp.int32) - 1
    got_label = (row_ids // slot_rows) * entries + got[:, features + 1].astype(jnp.int32)
    place = got_target[None, :] == jnp.arange(ROWS, dtype=jnp.int32)[:, None]
    packed = jnp.dot(
        place.astype(frames.dtype), got[:, :features], preferred_element_type=jnp.float32
    ).astype(frames.dtype)
    packed_labels = jnp.max(jnp.where(place, got_label[None, :], -1), axis=1)
    hidden = jnp.dot(packed, in_weight, preferred_element_type=jnp.float32).astype(jnp.bfloat16)
    hidden_wide = hidden.astype(jnp.float32)
    taps = depth_weight.astype(jnp.float32)
    convolved = depth_conv(hidden_wide, taps, packed_labels, 1)
    activated = jax.nn.silu(convolved).astype(jnp.bfloat16)
    partial_sum = lax.dot_general(
        activated, out_weight, (((1,), (1,)), ((), ())), preferred_element_type=jnp.float32
    )
    mp_count = lax.axis_size("mp")
    width = out_weight.shape[1]
    block_sums = partial_sum.astype(jnp.bfloat16).reshape(ROWS, mp_count, width)
    branch_parts = lax.all_to_all(
        jnp.swapaxes(block_sums, 0, 1), "mp", split_axis=0, concat_axis=0, tiled=True
    )
    branch = jnp.sum(branch_parts.astype(jnp.float32), axis=0)
    output = (hidden_wide + branch).astype(jnp.bfloat16)
    model_index = lax.axis_index("mp")
    shifted = [cotangent] + [
        lax.ppermute(cotangent, "mp", [(m, (m + k) % mp_count) for m in range(mp_count)])
        for k in range(1, mp_count)
    ]
    order = (model_index - jnp.arange(mp_count, dtype=jnp.int32)) % mp_count
    cotangent_blocks = jnp.take(jnp.stack(shifted, axis=0), order, axis=0)
    weight_blocks = out_weight.reshape(mp_count, width, width)
    grad_scale = 1.0 / math.sqrt(dp_count * ROWS)
    grad_activated = jnp.einsum(
        "mtc,mci->ti", cotangent_blocks, weight_blocks, preferred_element_type=jnp.float32
    )
    sigmoid_value = jax.nn.sigmoid(convolved)
    grad_convolved = grad_activated * sigmoid_value * (1.0 + convolved * (1.0 - sigmoid_value))
    grad_hidden = (
        cotangent.astype(jnp.float32) + depth_conv(grad_convolved, taps, packed_labels, -1)
    ).astype(jnp.bfloat16)
    term_out = grad_scale * jnp.einsum(
        "mtc,ti->mci", cotangent_blocks, activated, preferred_element_type=jnp.float32
    )
    term_in = grad_scale * lax.dot_general(
        packed, grad_hidden, (((0,), (0,)), ((), ())), preferred_element_type=jnp.float32
    )
    term_depth = grad_scale * tap_sums(grad_convolved, hidden_wide, packed_labels)
    out_rows = term_out.shape[0] * term_out.shape[1] // dp_count
    small = jnp.concatenate((term_in, term_depth), axis=0)
    small_rows = -(-small.shape[0] // dp_count)
    small = jnp.pad(small, ((0, small_rows * dp_count - small.shape[0]), (0, 0)))
    combined = jnp.concatenate(
        (
            term_out.reshape(dp_count, out_rows, width),
            small.reshape(dp_count, small_rows, width),
        ),
        axis=1,
    )
    core = lax.axis_index(DP[-1])
    cores = lax.axis_size(DP[-1])
    paired = combined.reshape((dp_count // cores, cores) + combined.shape[1:])
    keep = jnp.where(core == 0, paired[:, 0], paired[:, 1])
    give = jnp.where(core == 0, paired[:, 1], paired[:, 0])
    pair_sum = keep + lax.ppermute(give, DP[-1], [(0, 1), (1, 0)])
    exchanged = lax.all_to_all(pair_sum, DP[:-1], split_axis=0, concat_axis=0, tiled=True)
    reduced = jnp.sum(exchanged, axis=0)
    out_weight_gradient = reduced[:out_rows]
    piece = reduced[out_rows:].astype(jnp.bfloat16)
    sibling = lax.ppermute(piece, DP[-1], [(0, 1), (1, 0)])
    pair_piece = jnp.where(
        core == 0, jnp.stack((piece, sibling), 0), jnp.stack((sibling, piece), 0)
    )
    spread = jnp.broadcast_to(pair_piece[None], (dp_count // cores,) + pair_piece.shape)
    gathered = lax.all_to_all(spread, DP[:-1], split_axis=0, concat_axis=0, tiled=True)
    small_full = gathered.reshape(dp_count * small_rows, width).astype(jnp.float32)
    in_rows = term_in.shape[0]
    in_weight_gradient = small_full[:in_rows]
    depth_gradient = small_full[in_rows : in_rows + term_depth.shape[0]]
    return (output, in_weight_gradient, depth_gradient, out_weight_gradient)


def split_mesh(mesh):
    devices = mesh.devices
    column = devices[:, 0]
    ys = len({device.coords[1] for device in column})
    zs = len({device.coords[2] for device in column})
    cores = devices.shape[0] // (ys * zs)
    return jax.sharding.Mesh(devices.reshape(ys, zs, cores, devices.shape[1]), DP + ("mp",))


def solution(mesh):
    placed = (
        P(DP, None),
        P(DP, None),
        P(DP, None),
        P(DP, None),
        P(None, "mp"),
        P(None, "mp"),
        P(None, "mp"),
        P(DP, "mp"),
    )
    return jax.shard_map(
        per_device,
        mesh=split_mesh(mesh),
        in_specs=placed,
        out_specs=(P(DP, "mp"), P(None, "mp"), P(None, "mp"), P(DP, "mp")),
        check_vma=False,
    )
```

```python
import math

import jax
import jax.numpy as jnp
from jax import lax
from jax.sharding import PartitionSpec as P

KERNEL = 31
ROWS = 256
DP = ("y", "z", "core")


def depth_conv(values, weights, labels, direction):
    center = (KERNEL - 1) // 2
    length = values.shape[0]
    padded = jnp.pad(values, ((center, center), (0, 0)))
    padded_labels = jnp.pad(labels, (center, center), constant_values=-1)
    result = jnp.zeros(values.shape, jnp.float32)
    for tap_index in range(KERNEL):
        start = center + direction * (tap_index - center)
        matches = (padded_labels[start : start + length] == labels)[:, None]
        taken = weights[tap_index][None, :] * padded[start : start + length]
        result = result + jnp.where(matches, taken, jnp.zeros_like(taken))
    return result


def tap_sums(grads, values, labels):
    center = (KERNEL - 1) // 2
    length = values.shape[0]
    padded = jnp.pad(values, ((center, center), (0, 0)))
    padded_labels = jnp.pad(labels, (center, center), constant_values=-1)
    rows_list = []
    for tap_index in range(KERNEL):
        matches = (padded_labels[tap_index : tap_index + length] == labels)[:, None]
        taken = grads * padded[tap_index : tap_index + length]
        rows_list.append(jnp.sum(jnp.where(matches, taken, jnp.zeros_like(taken)), axis=0))
    return jnp.stack(rows_list, 0)


def per_device(
    frames, lengths, destinations, offsets, in_weight, depth_weight, out_weight, cotangent
):
    dp_count = lax.axis_size(DP)
    src_rows = frames.shape[0]
    features = frames.shape[1]
    slot_rows = src_rows // dp_count
    entries = lengths.shape[1]
    lengths_row = lengths[0]
    end_rows = jnp.cumsum(lengths_row, dtype=jnp.int32)
    begins = end_rows - lengths_row
    row_ids = jnp.arange(src_rows, dtype=jnp.int32)
    owner_table = (begins[None, :] <= row_ids[:, None]) & (row_ids[:, None] < end_rows[None, :])
    occupied_rows = jnp.any(owner_table, axis=1)

    def lookup(table):
        return jnp.sum(jnp.where(owner_table, table[None, :], 0), axis=1, dtype=jnp.int32)

    entry_ids = jnp.arange(entries, dtype=jnp.int32)
    owner = lookup(entry_ids)
    target = lookup(offsets[0] - begins) + row_ids + 1
    block_ids = jnp.arange(dp_count, dtype=jnp.int32)
    block_dest = jnp.where(occupied_rows, lookup(destinations[0]), -1)[::slot_rows]
    chosen = block_dest[None, :] == block_ids[:, None]
    block_of = jnp.where(
        jnp.any(chosen, axis=1), jnp.sum(jnp.where(chosen, block_ids[None, :], 0), axis=1), dp_count
    )
    codes = jnp.stack((jnp.where(occupied_rows, target, 0), owner), axis=1).astype(frames.dtype)
    blocks = jnp.concatenate((frames, codes), axis=1)
    blocks = jnp.concatenate((blocks, jnp.zeros((slot_rows, features + 2), frames.dtype)), axis=0)
    send = jnp.take(
        blocks.reshape(dp_count + 1, slot_rows, features + 2), block_of, axis=0, mode="clip"
    )
    got = lax.all_to_all(send, DP, split_axis=0, concat_axis=0, tiled=True)
    got = got.reshape(dp_count * slot_rows, features + 2)
    got_target = got[:, features].astype(jnp.int32) - 1
    got_label = (row_ids // slot_rows) * entries + got[:, features + 1].astype(jnp.int32)
    place = got_target[None, :] == jnp.arange(ROWS, dtype=jnp.int32)[:, None]
    packed = jnp.dot(
        place.astype(frames.dtype), got[:, :features], preferred_element_type=jnp.float32
    ).astype(frames.dtype)
    packed_labels = jnp.max(jnp.where(place, got_label[None, :], -1), axis=1)
    hidden = jnp.dot(packed, in_weight, preferred_element_type=jnp.float32).astype(jnp.bfloat16)
    hidden_wide = hidden.astype(jnp.float32)
    taps = depth_weight.astype(jnp.float32)
    convolved = depth_conv(hidden_wide, taps, packed_labels, 1)
    activated = jax.nn.silu(convolved).astype(jnp.bfloat16)
    partial_sum = lax.dot_general(
        activated, out_weight, (((1,), (1,)), ((), ())), preferred_element_type=jnp.float32
    )
    mp_count = lax.axis_size("mp")
    width = out_weight.shape[1]
    block_sums = partial_sum.astype(jnp.bfloat16).reshape(ROWS, mp_count, width)
    branch_parts = lax.all_to_all(
        jnp.swapaxes(block_sums, 0, 1), "mp", split_axis=0, concat_axis=0, tiled=True
    )
    branch = jnp.sum(branch_parts.astype(jnp.float32), axis=0)
    output = (hidden_wide + branch).astype(jnp.bfloat16)
    model_index = lax.axis_index("mp")
    shifted = [cotangent] + [
        lax.ppermute(cotangent, "mp", [(m, (m + k) % mp_count) for m in range(mp_count)])
        for k in range(1, mp_count)
    ]
    order = (model_index - jnp.arange(mp_count, dtype=jnp.int32)) % mp_count
    cotangent_blocks = jnp.take(jnp.stack(shifted, axis=0), order, axis=0)
    weight_blocks = out_weight.reshape(mp_count, width, width)
    grad_scale = 1.0 / math.sqrt(dp_count * ROWS)
    grad_activated = jnp.einsum(
        "mtc,mci->ti", cotangent_blocks, weight_blocks, preferred_element_type=jnp.float32
    )
    sigmoid_value = jax.nn.sigmoid(convolved)
    grad_convolved = grad_activated * sigmoid_value * (1.0 + convolved * (1.0 - sigmoid_value))
    grad_hidden = (
        cotangent.astype(jnp.float32) + depth_conv(grad_convolved, taps, packed_labels, -1)
    ).astype(jnp.bfloat16)
    term_out = grad_scale * jnp.einsum(
        "mtc,ti->mci", cotangent_blocks, activated, preferred_element_type=jnp.float32
    )
    term_in = grad_scale * lax.dot_general(
        packed, grad_hidden, (((0,), (0,)), ((), ())), preferred_element_type=jnp.float32
    )
    term_depth = grad_scale * tap_sums(grad_convolved, hidden_wide, packed_labels)
    out_rows = term_out.shape[0] * term_out.shape[1] // dp_count
    small = jnp.concatenate((term_in, term_depth), axis=0)
    small_rows = -(-small.shape[0] // dp_count)
    small = jnp.pad(small, ((0, small_rows * dp_count - small.shape[0]), (0, 0)))
    combined = jnp.concatenate(
        (
            term_out.reshape(dp_count, out_rows, width),
            small.reshape(dp_count, small_rows, width),
        ),
        axis=1,
    )
    core = lax.axis_index(DP[-1])
    cores = lax.axis_size(DP[-1])
    paired = combined.reshape((dp_count // cores, cores) + combined.shape[1:])
    keep = jnp.where(core == 0, paired[:, 0], paired[:, 1])
    give = jnp.where(core == 0, paired[:, 1], paired[:, 0])
    pair_sum = keep + lax.ppermute(give, DP[-1], [(0, 1), (1, 0)])
    exchanged = lax.all_to_all(pair_sum, DP[:-1], split_axis=0, concat_axis=0, tiled=True)
    reduced = jnp.sum(exchanged, axis=0)
    out_weight_gradient = reduced[:out_rows]
    spread = jnp.broadcast_to(
        reduced[out_rows:].astype(jnp.bfloat16)[None], (dp_count, small_rows, width)
    )
    gathered = lax.all_to_all(spread, DP, split_axis=0, concat_axis=0, tiled=True)
    small_full = gathered.reshape(dp_count * small_rows, width).astype(jnp.float32)
    in_rows = term_in.shape[0]
    in_weight_gradient = small_full[:in_rows]
    depth_gradient = small_full[in_rows : in_rows + term_depth.shape[0]]
    return (output, in_weight_gradient, depth_gradient, out_weight_gradient)


def split_mesh(mesh):
    devices = mesh.devices
    column = devices[:, 0]
    ys = len({device.coords[1] for device in column})
    zs = len({device.coords[2] for device in column})
    cores = devices.shape[0] // (ys * zs)
    return jax.sharding.Mesh(devices.reshape(ys, zs, cores, devices.shape[1]), DP + ("mp",))


def solution(mesh):
    placed = (
        P(DP, None),
        P(DP, None),
        P(DP, None),
        P(DP, None),
        P(None, "mp"),
        P(None, "mp"),
        P(None, "mp"),
        P(DP, "mp"),
    )
    return jax.shard_map(
        per_device,
        mesh=split_mesh(mesh),
        in_specs=placed,
        out_specs=(P(DP, "mp"), P(None, "mp"), P(None, "mp"), P(DP, "mp")),
        check_vma=False,
    )
```

```python
import math

import jax
import jax.numpy as jnp
from jax import lax
from jax.sharding import PartitionSpec as P

KERNEL = 31
ROWS = 256
DP = ("y", "z", "core")


def depth_conv(values, weights, labels, direction):
    center = (KERNEL - 1) // 2
    length = values.shape[0]
    padded = jnp.pad(values, ((center, center), (0, 0)))
    padded_labels = jnp.pad(labels, (center, center), constant_values=-1)
    result = jnp.zeros(values.shape, jnp.float32)
    for tap_index in range(KERNEL):
        start = center + direction * (tap_index - center)
        matches = (padded_labels[start : start + length] == labels)[:, None]
        taken = weights[tap_index][None, :] * padded[start : start + length]
        result = result + jnp.where(matches, taken, jnp.zeros_like(taken))
    return result


def tap_sums(grads, values, labels):
    center = (KERNEL - 1) // 2
    length = values.shape[0]
    padded = jnp.pad(values, ((center, center), (0, 0)))
    padded_labels = jnp.pad(labels, (center, center), constant_values=-1)
    rows_list = []
    for tap_index in range(KERNEL):
        matches = (padded_labels[tap_index : tap_index + length] == labels)[:, None]
        taken = grads * padded[tap_index : tap_index + length]
        rows_list.append(jnp.sum(jnp.where(matches, taken, jnp.zeros_like(taken)), axis=0))
    return jnp.stack(rows_list, 0)


def per_device(
    frames, lengths, destinations, offsets, in_weight, depth_weight, out_weight, cotangent
):
    dp_count = lax.axis_size(DP)
    src_rows = frames.shape[0]
    features = frames.shape[1]
    slot_rows = src_rows // dp_count
    entries = lengths.shape[1]
    lengths_row = lengths[0]
    end_rows = jnp.cumsum(lengths_row, dtype=jnp.int32)
    begins = end_rows - lengths_row
    row_ids = jnp.arange(src_rows, dtype=jnp.int32)
    owner_table = (begins[None, :] <= row_ids[:, None]) & (row_ids[:, None] < end_rows[None, :])
    occupied_rows = jnp.any(owner_table, axis=1)

    def lookup(table):
        return jnp.sum(jnp.where(owner_table, table[None, :], 0), axis=1, dtype=jnp.int32)

    entry_ids = jnp.arange(entries, dtype=jnp.int32)
    owner = lookup(entry_ids)
    target = lookup(offsets[0] - begins) + row_ids + 1
    block_ids = jnp.arange(dp_count, dtype=jnp.int32)
    block_dest = jnp.where(occupied_rows, lookup(destinations[0]), -1)[::slot_rows]
    chosen = block_dest[None, :] == block_ids[:, None]
    block_of = jnp.where(
        jnp.any(chosen, axis=1), jnp.sum(jnp.where(chosen, block_ids[None, :], 0), axis=1), dp_count
    )
    codes = jnp.stack((jnp.where(occupied_rows, target, 0), owner), axis=1).astype(frames.dtype)
    blocks = jnp.concatenate((frames, codes), axis=1)
    blocks = jnp.concatenate((blocks, jnp.zeros((slot_rows, features + 2), frames.dtype)), axis=0)
    send = jnp.take(
        blocks.reshape(dp_count + 1, slot_rows, features + 2), block_of, axis=0, mode="clip"
    )
    got = lax.all_to_all(send, DP, split_axis=0, concat_axis=0, tiled=True)
    got = got.reshape(dp_count * slot_rows, features + 2)
    got_target = got[:, features].astype(jnp.int32) - 1
    got_label = (row_ids // slot_rows) * entries + got[:, features + 1].astype(jnp.int32)
    place = got_target[None, :] == jnp.arange(ROWS, dtype=jnp.int32)[:, None]
    packed = jnp.dot(
        place.astype(frames.dtype), got[:, :features], preferred_element_type=jnp.float32
    ).astype(frames.dtype)
    packed_labels = jnp.max(jnp.where(place, got_label[None, :], -1), axis=1)
    hidden = jnp.dot(packed, in_weight, preferred_element_type=jnp.float32).astype(jnp.bfloat16)
    hidden_wide = hidden.astype(jnp.float32)
    taps = depth_weight.astype(jnp.float32)
    convolved = depth_conv(hidden_wide, taps, packed_labels, 1)
    activated = jax.nn.silu(convolved).astype(jnp.bfloat16)
    partial_sum = lax.dot_general(
        activated, out_weight, (((1,), (1,)), ((), ())), preferred_element_type=jnp.float32
    )
    mp_count = lax.axis_size("mp")
    width = out_weight.shape[1]
    block_sums = partial_sum.astype(jnp.bfloat16).reshape(ROWS, mp_count, width)
    branch_parts = lax.all_to_all(
        jnp.swapaxes(block_sums, 0, 1), "mp", split_axis=0, concat_axis=0, tiled=True
    )
    branch = jnp.sum(branch_parts.astype(jnp.float32), axis=0)
    output = (hidden_wide + branch).astype(jnp.bfloat16)
    model_index = lax.axis_index("mp")
    shifted = [cotangent] + [
        lax.ppermute(cotangent, "mp", [(m, (m + k) % mp_count) for m in range(mp_count)])
        for k in range(1, mp_count)
    ]
    order = (model_index - jnp.arange(mp_count, dtype=jnp.int32)) % mp_count
    cotangent_blocks = jnp.take(jnp.stack(shifted, axis=0), order, axis=0)
    weight_blocks = out_weight.reshape(mp_count, width, width)
    grad_scale = 1.0 / math.sqrt(dp_count * ROWS)
    core = lax.axis_index(DP[-1])
    cores = lax.axis_size(DP[-1])

    def pair_sum_of(part):
        paired = part.reshape((dp_count // cores, cores) + part.shape[1:])
        keep = jnp.where(core == 0, paired[:, 0], paired[:, 1])
        give = jnp.where(core == 0, paired[:, 1], paired[:, 0])
        return keep + lax.ppermute(give, DP[-1], [(0, 1), (1, 0)])

    term_out = grad_scale * jnp.einsum(
        "mtc,ti->mci", cotangent_blocks, activated, preferred_element_type=jnp.float32
    )
    out_rows = term_out.shape[0] * term_out.shape[1] // dp_count
    out_pairs = pair_sum_of(term_out.reshape(dp_count, out_rows, width))
    grad_activated = jnp.einsum(
        "mtc,mci->ti", cotangent_blocks, weight_blocks, preferred_element_type=jnp.float32
    )
    sigmoid_value = jax.nn.sigmoid(convolved)
    grad_convolved = grad_activated * sigmoid_value * (1.0 + convolved * (1.0 - sigmoid_value))
    grad_hidden = (
        cotangent.astype(jnp.float32) + depth_conv(grad_convolved, taps, packed_labels, -1)
    ).astype(jnp.bfloat16)
    term_in = grad_scale * lax.dot_general(
        packed, grad_hidden, (((0,), (0,)), ((), ())), preferred_element_type=jnp.float32
    )
    term_depth = grad_scale * tap_sums(grad_convolved, hidden_wide, packed_labels)
    small = jnp.concatenate((term_in, term_depth), axis=0)
    small_rows = -(-small.shape[0] // dp_count)
    small = jnp.pad(small, ((0, small_rows * dp_count - small.shape[0]), (0, 0)))
    small_pairs = pair_sum_of(small.reshape(dp_count, small_rows, width))
    pair_sum = jnp.concatenate((out_pairs, small_pairs), axis=1)
    exchanged = lax.all_to_all(pair_sum, DP[:-1], split_axis=0, concat_axis=0, tiled=True)
    reduced = jnp.sum(exchanged, axis=0)
    out_weight_gradient = reduced[:out_rows]
    spread = jnp.broadcast_to(
        reduced[out_rows:].astype(jnp.bfloat16)[None], (dp_count, small_rows, width)
    )
    gathered = lax.all_to_all(spread, DP, split_axis=0, concat_axis=0, tiled=True)
    small_full = gathered.reshape(dp_count * small_rows, width).astype(jnp.float32)
    in_rows = term_in.shape[0]
    in_weight_gradient = small_full[:in_rows]
    depth_gradient = small_full[in_rows : in_rows + term_depth.shape[0]]
    return (output, in_weight_gradient, depth_gradient, out_weight_gradient)


def split_mesh(mesh):
    devices = mesh.devices
    column = devices[:, 0]
    ys = len({device.coords[1] for device in column})
    zs = len({device.coords[2] for device in column})
    cores = devices.shape[0] // (ys * zs)
    return jax.sharding.Mesh(devices.reshape(ys, zs, cores, devices.shape[1]), DP + ("mp",))


def solution(mesh):
    placed = (
        P(DP, None),
        P(DP, None),
        P(DP, None),
        P(DP, None),
        P(None, "mp"),
        P(None, "mp"),
        P(None, "mp"),
        P(DP, "mp"),
    )
    return jax.shard_map(
        per_device,
        mesh=split_mesh(mesh),
        in_specs=placed,
        out_specs=(P(DP, "mp"), P(None, "mp"), P(None, "mp"), P(DP, "mp")),
        check_vma=False,
    )
```

```python
import math

import jax
import jax.numpy as jnp
from jax import lax
from jax.sharding import PartitionSpec as P

KERNEL = 31
ROWS = 256
DP = ("y", "z", "core")


def depth_conv(values, weights, labels, direction):
    center = (KERNEL - 1) // 2
    length = values.shape[0]
    padded = jnp.pad(values, ((center, center), (0, 0)))
    padded_labels = jnp.pad(labels, (center, center), constant_values=-1)
    result = jnp.zeros(values.shape, jnp.float32)
    for tap_index in range(KERNEL):
        start = center + direction * (tap_index - center)
        matches = (padded_labels[start : start + length] == labels)[:, None]
        taken = weights[tap_index][None, :] * padded[start : start + length]
        result = result + jnp.where(matches, taken, jnp.zeros_like(taken))
    return result


def tap_sums(grads, values, labels):
    center = (KERNEL - 1) // 2
    length = values.shape[0]
    padded = jnp.pad(values, ((center, center), (0, 0)))
    padded_labels = jnp.pad(labels, (center, center), constant_values=-1)
    rows_list = []
    for tap_index in range(KERNEL):
        matches = (padded_labels[tap_index : tap_index + length] == labels)[:, None]
        taken = grads * padded[tap_index : tap_index + length]
        rows_list.append(jnp.sum(jnp.where(matches, taken, jnp.zeros_like(taken)), axis=0))
    return jnp.stack(rows_list, 0)


def per_device(
    frames, lengths, destinations, offsets, in_weight, depth_weight, out_weight, cotangent
):
    dp_count = lax.axis_size(DP)
    src_rows = frames.shape[0]
    features = frames.shape[1]
    slot_rows = src_rows // dp_count
    entries = lengths.shape[1]
    lengths_row = lengths[0]
    end_rows = jnp.cumsum(lengths_row, dtype=jnp.int32)
    begins = end_rows - lengths_row
    row_ids = jnp.arange(src_rows, dtype=jnp.int32)
    owner_table = (begins[None, :] <= row_ids[:, None]) & (row_ids[:, None] < end_rows[None, :])
    occupied_rows = jnp.any(owner_table, axis=1)

    def lookup(table):
        return jnp.sum(jnp.where(owner_table, table[None, :], 0), axis=1, dtype=jnp.int32)

    entry_ids = jnp.arange(entries, dtype=jnp.int32)
    owner = lookup(entry_ids)
    target = lookup(offsets[0] - begins) + row_ids + 1
    block_ids = jnp.arange(dp_count, dtype=jnp.int32)
    block_dest = jnp.where(occupied_rows, lookup(destinations[0]), -1)[::slot_rows]
    chosen = block_dest[None, :] == block_ids[:, None]
    block_of = jnp.where(
        jnp.any(chosen, axis=1), jnp.sum(jnp.where(chosen, block_ids[None, :], 0), axis=1), dp_count
    )
    codes = jnp.stack((jnp.where(occupied_rows, target, 0), owner), axis=1).astype(frames.dtype)
    blocks = jnp.concatenate((frames, codes), axis=1)
    blocks = jnp.concatenate((blocks, jnp.zeros((slot_rows, features + 2), frames.dtype)), axis=0)
    send = jnp.take(
        blocks.reshape(dp_count + 1, slot_rows, features + 2), block_of, axis=0, mode="clip"
    )
    got = lax.all_to_all(send, DP, split_axis=0, concat_axis=0, tiled=True)
    got = got.reshape(dp_count * slot_rows, features + 2)
    got_target = got[:, features].astype(jnp.int32) - 1
    got_label = (row_ids // slot_rows) * entries + got[:, features + 1].astype(jnp.int32)
    place = got_target[None, :] == jnp.arange(ROWS, dtype=jnp.int32)[:, None]
    packed = jnp.dot(
        place.astype(frames.dtype), got[:, :features], preferred_element_type=jnp.float32
    ).astype(frames.dtype)
    packed_labels = jnp.max(jnp.where(place, got_label[None, :], -1), axis=1)
    hidden = jnp.dot(packed, in_weight, preferred_element_type=jnp.float32).astype(jnp.bfloat16)
    hidden_wide = hidden.astype(jnp.float32)
    taps = depth_weight.astype(jnp.float32)
    convolved = depth_conv(hidden_wide, taps, packed_labels, 1)
    activated = jax.nn.silu(convolved).astype(jnp.bfloat16)
    partial_sum = lax.dot_general(
        activated, out_weight, (((1,), (1,)), ((), ())), preferred_element_type=jnp.float32
    )
    mp_count = lax.axis_size("mp")
    width = out_weight.shape[1]
    block_sums = partial_sum.astype(jnp.bfloat16).reshape(ROWS, mp_count, width)
    branch_parts = lax.all_to_all(
        jnp.swapaxes(block_sums, 0, 1), "mp", split_axis=0, concat_axis=0, tiled=True
    )
    branch = jnp.sum(branch_parts.astype(jnp.float32), axis=0)
    output = (hidden_wide + branch).astype(jnp.bfloat16)
    model_index = lax.axis_index("mp")
    shifted = [cotangent] + [
        lax.ppermute(cotangent, "mp", [(m, (m + k) % mp_count) for m in range(mp_count)])
        for k in range(1, mp_count)
    ]
    order = (model_index - jnp.arange(mp_count, dtype=jnp.int32)) % mp_count
    cotangent_blocks = jnp.take(jnp.stack(shifted, axis=0), order, axis=0)
    weight_blocks = out_weight.reshape(mp_count, width, width)
    grad_scale = 1.0 / math.sqrt(dp_count * ROWS)
    grad_activated = jnp.einsum(
        "mtc,mci->ti", cotangent_blocks, weight_blocks, preferred_element_type=jnp.float32
    )
    sigmoid_value = jax.nn.sigmoid(convolved)
    grad_convolved = grad_activated * sigmoid_value * (1.0 + convolved * (1.0 - sigmoid_value))
    grad_hidden = (
        cotangent.astype(jnp.float32) + depth_conv(grad_convolved, taps, packed_labels, -1)
    ).astype(jnp.bfloat16)
    term_out = grad_scale * jnp.einsum(
        "mtc,ti->mci", cotangent_blocks, activated, preferred_element_type=jnp.float32
    )
    term_in = grad_scale * lax.dot_general(
        packed, grad_hidden, (((0,), (0,)), ((), ())), preferred_element_type=jnp.float32
    )
    term_depth = grad_scale * tap_sums(grad_convolved, hidden_wide, packed_labels)
    out_rows = term_out.shape[0] * term_out.shape[1] // dp_count
    small = jnp.concatenate((term_in, term_depth), axis=0)
    small_rows = -(-small.shape[0] // dp_count)
    small = jnp.pad(small, ((0, small_rows * dp_count - small.shape[0]), (0, 0)))
    combined = jnp.concatenate(
        (
            term_out.reshape(dp_count, out_rows, width),
            small.reshape(dp_count, small_rows, width),
        ),
        axis=1,
    )
    core = lax.axis_index(DP[-1])
    cores = lax.axis_size(DP[-1])
    paired = combined.reshape((dp_count // cores, cores) + combined.shape[1:])
    keep = lax.dynamic_index_in_dim(paired, core, 1, keepdims=False)
    give = lax.dynamic_index_in_dim(paired, 1 - core, 1, keepdims=False)
    pair_sum = keep + lax.ppermute(give, DP[-1], [(0, 1), (1, 0)])
    exchanged = lax.all_to_all(pair_sum, DP[:-1], split_axis=0, concat_axis=0, tiled=True)
    reduced = jnp.sum(exchanged, axis=0)
    out_weight_gradient = reduced[:out_rows]
    spread = jnp.broadcast_to(
        reduced[out_rows:].astype(jnp.bfloat16)[None], (dp_count, small_rows, width)
    )
    gathered = lax.all_to_all(spread, DP, split_axis=0, concat_axis=0, tiled=True)
    small_full = gathered.reshape(dp_count * small_rows, width).astype(jnp.float32)
    in_rows = term_in.shape[0]
    in_weight_gradient = small_full[:in_rows]
    depth_gradient = small_full[in_rows : in_rows + term_depth.shape[0]]
    return (output, in_weight_gradient, depth_gradient, out_weight_gradient)


def split_mesh(mesh):
    devices = mesh.devices
    column = devices[:, 0]
    ys = len({device.coords[1] for device in column})
    zs = len({device.coords[2] for device in column})
    cores = devices.shape[0] // (ys * zs)
    return jax.sharding.Mesh(devices.reshape(ys, zs, cores, devices.shape[1]), DP + ("mp",))


def solution(mesh):
    placed = (
        P(DP, None),
        P(DP, None),
        P(DP, None),
        P(DP, None),
        P(None, "mp"),
        P(None, "mp"),
        P(None, "mp"),
        P(DP, "mp"),
    )
    return jax.shard_map(
        per_device,
        mesh=split_mesh(mesh),
        in_specs=placed,
        out_specs=(P(DP, "mp"), P(None, "mp"), P(None, "mp"), P(DP, "mp")),
        check_vma=False,
    )
```

```python
import math

import jax
import jax.numpy as jnp
from jax import lax
from jax.sharding import PartitionSpec as P

KERNEL = 31
ROWS = 256
DP = ("y", "z", "core")


def depth_conv(values, weights, labels, direction):
    center = (KERNEL - 1) // 2
    length = values.shape[0]
    padded = jnp.pad(values, ((center, center), (0, 0)))
    padded_labels = jnp.pad(labels, (center, center), constant_values=-1)
    result = jnp.zeros(values.shape, jnp.float32)
    for tap_index in range(KERNEL):
        start = center + direction * (tap_index - center)
        matches = (padded_labels[start : start + length] == labels)[:, None]
        taken = weights[tap_index][None, :] * padded[start : start + length]
        result = result + jnp.where(matches, taken, jnp.zeros_like(taken))
    return result


def tap_sums(grads, values, labels):
    center = (KERNEL - 1) // 2
    length = values.shape[0]
    padded = jnp.pad(values, ((center, center), (0, 0)))
    padded_labels = jnp.pad(labels, (center, center), constant_values=-1)
    rows_list = []
    for tap_index in range(KERNEL):
        matches = (padded_labels[tap_index : tap_index + length] == labels)[:, None]
        taken = grads * padded[tap_index : tap_index + length]
        rows_list.append(jnp.sum(jnp.where(matches, taken, jnp.zeros_like(taken)), axis=0))
    return jnp.stack(rows_list, 0)


def per_device(
    frames, lengths, destinations, offsets, in_weight, depth_weight, out_weight, cotangent
):
    dp_count = lax.axis_size(DP)
    src_rows = frames.shape[0]
    features = frames.shape[1]
    slot_rows = src_rows // dp_count
    entries = lengths.shape[1]
    lengths_row = lengths[0]
    end_rows = jnp.cumsum(lengths_row, dtype=jnp.int32)
    begins = end_rows - lengths_row
    row_ids = jnp.arange(src_rows, dtype=jnp.int32)
    owner_table = (begins[None, :] <= row_ids[:, None]) & (row_ids[:, None] < end_rows[None, :])
    occupied_rows = jnp.any(owner_table, axis=1)

    def lookup(table):
        return jnp.sum(jnp.where(owner_table, table[None, :], 0), axis=1, dtype=jnp.int32)

    entry_ids = jnp.arange(entries, dtype=jnp.int32)
    owner = lookup(entry_ids)
    target = lookup(offsets[0] - begins) + row_ids + 1
    block_ids = jnp.arange(dp_count, dtype=jnp.int32)
    block_dest = jnp.where(occupied_rows, lookup(destinations[0]), -1)[::slot_rows]
    chosen = block_dest[None, :] == block_ids[:, None]
    block_of = jnp.where(
        jnp.any(chosen, axis=1), jnp.sum(jnp.where(chosen, block_ids[None, :], 0), axis=1), dp_count
    )
    codes = jnp.stack((jnp.where(occupied_rows, target, 0), owner), axis=1).astype(frames.dtype)
    blocks = jnp.concatenate((frames, codes), axis=1)
    blocks = jnp.concatenate((blocks, jnp.zeros((slot_rows, features + 2), frames.dtype)), axis=0)
    send = jnp.take(
        blocks.reshape(dp_count + 1, slot_rows, features + 2), block_of, axis=0, mode="clip"
    )
    got = lax.all_to_all(send, DP, split_axis=0, concat_axis=0, tiled=True)
    got = got.reshape(dp_count * slot_rows, features + 2)
    got_target = got[:, features].astype(jnp.int32) - 1
    got_label = (row_ids // slot_rows) * entries + got[:, features + 1].astype(jnp.int32)
    place = got_target[None, :] == jnp.arange(ROWS, dtype=jnp.int32)[:, None]
    packed = jnp.dot(
        place.astype(frames.dtype), got[:, :features], preferred_element_type=jnp.float32
    ).astype(frames.dtype)
    packed_labels = jnp.max(jnp.where(place, got_label[None, :], -1), axis=1)
    hidden = jnp.dot(packed, in_weight, preferred_element_type=jnp.float32).astype(jnp.bfloat16)
    hidden_wide = hidden.astype(jnp.float32)
    taps = depth_weight.astype(jnp.float32)
    convolved = depth_conv(hidden_wide, taps, packed_labels, 1)
    activated = jax.nn.silu(convolved).astype(jnp.bfloat16)
    mp_count = lax.axis_size("mp")
    width = out_weight.shape[1]
    block_sums = jnp.einsum(
        "tc,mic->mti",
        activated,
        out_weight.reshape(mp_count, width, width),
        preferred_element_type=jnp.float32,
    ).astype(jnp.bfloat16)
    branch_parts = lax.all_to_all(block_sums, "mp", split_axis=0, concat_axis=0, tiled=True)
    branch = jnp.sum(branch_parts.astype(jnp.float32), axis=0)
    output = (hidden_wide + branch).astype(jnp.bfloat16)
    model_index = lax.axis_index("mp")
    shifted = [cotangent] + [
        lax.ppermute(cotangent, "mp", [(m, (m + k) % mp_count) for m in range(mp_count)])
        for k in range(1, mp_count)
    ]
    order = (model_index - jnp.arange(mp_count, dtype=jnp.int32)) % mp_count
    cotangent_blocks = jnp.take(jnp.stack(shifted, axis=0), order, axis=0)
    weight_blocks = out_weight.reshape(mp_count, width, width)
    grad_scale = 1.0 / math.sqrt(dp_count * ROWS)
    grad_activated = jnp.einsum(
        "mtc,mci->ti", cotangent_blocks, weight_blocks, preferred_element_type=jnp.float32
    )
    sigmoid_value = jax.nn.sigmoid(convolved)
    grad_convolved = grad_activated * sigmoid_value * (1.0 + convolved * (1.0 - sigmoid_value))
    grad_hidden = (
        cotangent.astype(jnp.float32) + depth_conv(grad_convolved, taps, packed_labels, -1)
    ).astype(jnp.bfloat16)
    term_out = grad_scale * jnp.einsum(
        "mtc,ti->mci", cotangent_blocks, activated, preferred_element_type=jnp.float32
    )
    term_in = grad_scale * lax.dot_general(
        packed, grad_hidden, (((0,), (0,)), ((), ())), preferred_element_type=jnp.float32
    )
    term_depth = grad_scale * tap_sums(grad_convolved, hidden_wide, packed_labels)
    out_rows = term_out.shape[0] * term_out.shape[1] // dp_count
    small = jnp.concatenate((term_in, term_depth), axis=0)
    small_rows = -(-small.shape[0] // dp_count)
    small = jnp.pad(small, ((0, small_rows * dp_count - small.shape[0]), (0, 0)))
    combined = jnp.concatenate(
        (
            term_out.reshape(dp_count, out_rows, width),
            small.reshape(dp_count, small_rows, width),
        ),
        axis=1,
    )
    core = lax.axis_index(DP[-1])
    cores = lax.axis_size(DP[-1])
    paired = combined.reshape((dp_count // cores, cores) + combined.shape[1:])
    keep = lax.dynamic_index_in_dim(paired, core, 1, keepdims=False)
    give = lax.dynamic_index_in_dim(paired, 1 - core, 1, keepdims=False)
    pair_sum = keep + lax.ppermute(give, DP[-1], [(0, 1), (1, 0)])
    exchanged = lax.all_to_all(pair_sum, DP[:-1], split_axis=0, concat_axis=0, tiled=True)
    reduced = jnp.sum(exchanged, axis=0)
    out_weight_gradient = reduced[:out_rows]
    spread = jnp.broadcast_to(
        reduced[out_rows:].astype(jnp.bfloat16)[None], (dp_count, small_rows, width)
    )
    gathered = lax.all_to_all(spread, DP, split_axis=0, concat_axis=0, tiled=True)
    small_full = gathered.reshape(dp_count * small_rows, width).astype(jnp.float32)
    in_rows = term_in.shape[0]
    in_weight_gradient = small_full[:in_rows]
    depth_gradient = small_full[in_rows : in_rows + term_depth.shape[0]]
    return (output, in_weight_gradient, depth_gradient, out_weight_gradient)


def split_mesh(mesh):
    devices = mesh.devices
    column = devices[:, 0]
    ys = len({device.coords[1] for device in column})
    zs = len({device.coords[2] for device in column})
    cores = devices.shape[0] // (ys * zs)
    return jax.sharding.Mesh(devices.reshape(ys, zs, cores, devices.shape[1]), DP + ("mp",))


def solution(mesh):
    placed = (
        P(DP, None),
        P(DP, None),
        P(DP, None),
        P(DP, None),
        P(None, "mp"),
        P(None, "mp"),
        P(None, "mp"),
        P(DP, "mp"),
    )
    return jax.shard_map(
        per_device,
        mesh=split_mesh(mesh),
        in_specs=placed,
        out_specs=(P(DP, "mp"), P(None, "mp"), P(None, "mp"), P(DP, "mp")),
        check_vma=False,
    )
```

```python
import math

import jax
import jax.numpy as jnp
from jax import lax
from jax.sharding import PartitionSpec as P

KERNEL = 31
ROWS = 256
DP = ("y", "z", "core")


def depth_conv(values, weights, labels, direction):
    center = (KERNEL - 1) // 2
    length = values.shape[0]
    padded = jnp.pad(values, ((center, center), (0, 0)))
    padded_labels = jnp.pad(labels, (center, center), constant_values=-1)
    result = jnp.zeros(values.shape, jnp.float32)
    for tap_index in range(KERNEL):
        start = center + direction * (tap_index - center)
        matches = (padded_labels[start : start + length] == labels)[:, None]
        taken = weights[tap_index][None, :] * padded[start : start + length]
        result = result + jnp.where(matches, taken, jnp.zeros_like(taken))
    return result


def tap_sums(grads, values, labels):
    center = (KERNEL - 1) // 2
    length = values.shape[0]
    padded = jnp.pad(values, ((center, center), (0, 0)))
    padded_labels = jnp.pad(labels, (center, center), constant_values=-1)
    rows_list = []
    for tap_index in range(KERNEL):
        matches = (padded_labels[tap_index : tap_index + length] == labels)[:, None]
        taken = grads * padded[tap_index : tap_index + length]
        rows_list.append(jnp.sum(jnp.where(matches, taken, jnp.zeros_like(taken)), axis=0))
    return jnp.stack(rows_list, 0)


def per_device(
    frames, lengths, destinations, offsets, in_weight, depth_weight, out_weight, cotangent
):
    dp_count = lax.axis_size(DP)
    src_rows = frames.shape[0]
    features = frames.shape[1]
    slot_rows = src_rows // dp_count
    entries = lengths.shape[1]
    lengths_row = lengths[0]
    end_rows = jnp.cumsum(lengths_row, dtype=jnp.int32)
    begins = end_rows - lengths_row
    row_ids = jnp.arange(src_rows, dtype=jnp.int32)
    owner_table = (begins[None, :] <= row_ids[:, None]) & (row_ids[:, None] < end_rows[None, :])
    occupied_rows = jnp.any(owner_table, axis=1)

    def lookup(table):
        return jnp.sum(jnp.where(owner_table, table[None, :], 0), axis=1, dtype=jnp.int32)

    entry_ids = jnp.arange(entries, dtype=jnp.int32)
    owner = lookup(entry_ids)
    target = lookup(offsets[0] - begins) + row_ids + 1
    block_ids = jnp.arange(dp_count, dtype=jnp.int32)
    block_dest = jnp.where(occupied_rows, lookup(destinations[0]), -1)[::slot_rows]
    chosen = block_dest[None, :] == block_ids[:, None]
    block_of = jnp.where(
        jnp.any(chosen, axis=1), jnp.sum(jnp.where(chosen, block_ids[None, :], 0), axis=1), dp_count
    )
    codes = jnp.stack((jnp.where(occupied_rows, target, 0), owner), axis=1).astype(frames.dtype)
    blocks = jnp.concatenate((frames, codes), axis=1)
    blocks = jnp.concatenate((blocks, jnp.zeros((slot_rows, features + 2), frames.dtype)), axis=0)
    send = jnp.take(
        blocks.reshape(dp_count + 1, slot_rows, features + 2), block_of, axis=0, mode="clip"
    )
    got = lax.all_to_all(send, DP, split_axis=0, concat_axis=0, tiled=True)
    got = got.reshape(dp_count * slot_rows, features + 2)
    got_target = got[:, features].astype(jnp.int32) - 1
    got_label = (row_ids // slot_rows) * entries + got[:, features + 1].astype(jnp.int32)
    place = got_target[None, :] == jnp.arange(ROWS, dtype=jnp.int32)[:, None]
    packed = jnp.dot(
        place.astype(frames.dtype), got[:, :features], preferred_element_type=jnp.float32
    ).astype(frames.dtype)
    packed_labels = jnp.max(jnp.where(place, got_label[None, :], -1), axis=1)
    hidden = jnp.dot(packed, in_weight, preferred_element_type=jnp.float32).astype(jnp.bfloat16)
    hidden_wide = hidden.astype(jnp.float32)
    taps = depth_weight.astype(jnp.float32)
    convolved = depth_conv(hidden_wide, taps, packed_labels, 1)
    activated = jax.nn.silu(convolved).astype(jnp.bfloat16)
    partial_sum = lax.dot_general(
        activated, out_weight, (((1,), (1,)), ((), ())), preferred_element_type=jnp.float32
    )
    mp_count = lax.axis_size("mp")
    width = out_weight.shape[1]
    block_sums = partial_sum.astype(jnp.bfloat16).reshape(ROWS, mp_count, width)
    branch_parts = lax.all_to_all(
        jnp.swapaxes(block_sums, 0, 1), "mp", split_axis=0, concat_axis=0, tiled=True
    )
    branch = jnp.sum(branch_parts.astype(jnp.float32), axis=0)
    output = (hidden_wide + branch).astype(jnp.bfloat16)
    model_index = lax.axis_index("mp")
    shifted = [cotangent] + [
        lax.ppermute(cotangent, "mp", [(m, (m + k) % mp_count) for m in range(mp_count)])
        for k in range(1, mp_count)
    ]
    order = (model_index - jnp.arange(mp_count, dtype=jnp.int32)) % mp_count
    cotangent_blocks = jnp.take(jnp.stack(shifted, axis=0), order, axis=0)
    weight_blocks = out_weight.reshape(mp_count, width, width)
    grad_scale = 1.0 / math.sqrt(dp_count * ROWS)
    grad_activated = jnp.einsum(
        "mtc,mci->ti", cotangent_blocks, weight_blocks, preferred_element_type=jnp.float32
    )
    sigmoid_value = jax.nn.sigmoid(convolved)
    grad_convolved = grad_activated * sigmoid_value * (1.0 + convolved * (1.0 - sigmoid_value))
    grad_hidden = (
        cotangent.astype(jnp.float32) + depth_conv(grad_convolved, taps, packed_labels, -1)
    ).astype(jnp.bfloat16)
    term_out = grad_scale * jnp.einsum(
        "mtc,ti->mci", cotangent_blocks, activated, preferred_element_type=jnp.float32
    )
    term_in = grad_scale * lax.dot_general(
        packed, grad_hidden, (((0,), (0,)), ((), ())), preferred_element_type=jnp.float32
    )
    term_depth = grad_scale * tap_sums(grad_convolved, hidden_wide, packed_labels)
    out_rows = term_out.shape[0] * term_out.shape[1] // dp_count
    small = jnp.concatenate((term_in, term_depth), axis=0)
    small_rows = -(-small.shape[0] // dp_count)
    small = jnp.pad(small, ((0, small_rows * dp_count - small.shape[0]), (0, 0)))
    combined = jnp.concatenate(
        (
            term_out.reshape(dp_count, out_rows, width),
            small.reshape(dp_count, small_rows, width),
        ),
        axis=1,
    )
    core = lax.axis_index(DP[-1])
    cores = lax.axis_size(DP[-1])
    paired = combined.reshape((dp_count // cores, cores) + combined.shape[1:])
    keep = lax.dynamic_index_in_dim(paired, core, 1, keepdims=False)
    give = lax.dynamic_index_in_dim(paired, 1 - core, 1, keepdims=False)
    pair_sum = keep + lax.ppermute(give, DP[-1], [(0, 1), (1, 0)])
    exchanged = lax.all_to_all(pair_sum, DP[:-1], split_axis=0, concat_axis=0, tiled=True)
    reduced = jnp.sum(exchanged, axis=0)
    out_weight_gradient = reduced[:out_rows]
    spread = jnp.broadcast_to(
        reduced[out_rows:][None], (dp_count, small_rows, width)
    )
    gathered = lax.all_to_all(spread, DP, split_axis=0, concat_axis=0, tiled=True)
    small_full = gathered.reshape(dp_count * small_rows, width)
    in_rows = term_in.shape[0]
    in_weight_gradient = small_full[:in_rows]
    depth_gradient = small_full[in_rows : in_rows + term_depth.shape[0]]
    return (output, in_weight_gradient, depth_gradient, out_weight_gradient)


def split_mesh(mesh):
    devices = mesh.devices
    column = devices[:, 0]
    ys = len({device.coords[1] for device in column})
    zs = len({device.coords[2] for device in column})
    cores = devices.shape[0] // (ys * zs)
    return jax.sharding.Mesh(devices.reshape(ys, zs, cores, devices.shape[1]), DP + ("mp",))


def solution(mesh):
    placed = (
        P(DP, None),
        P(DP, None),
        P(DP, None),
        P(DP, None),
        P(None, "mp"),
        P(None, "mp"),
        P(None, "mp"),
        P(DP, "mp"),
    )
    return jax.shard_map(
        per_device,
        mesh=split_mesh(mesh),
        in_specs=placed,
        out_specs=(P(DP, "mp"), P(None, "mp"), P(None, "mp"), P(DP, "mp")),
        check_vma=False,
    )
```

```python
import math

import jax
import jax.numpy as jnp
from jax import lax
from jax.sharding import PartitionSpec as P

KERNEL = 31
ROWS = 256
DP = ("y", "z", "core")


def depth_conv(values, weights, labels, direction):
    center = (KERNEL - 1) // 2
    length = values.shape[0]
    padded = jnp.pad(values, ((center, center), (0, 0)))
    padded_labels = jnp.pad(labels, (center, center), constant_values=-1)
    result = jnp.zeros(values.shape, jnp.float32)
    for tap_index in range(KERNEL):
        start = center + direction * (tap_index - center)
        matches = (padded_labels[start : start + length] == labels)[:, None]
        taken = weights[tap_index][None, :] * padded[start : start + length]
        result = result + jnp.where(matches, taken, jnp.zeros_like(taken))
    return result


def tap_sums(grads, values, labels):
    center = (KERNEL - 1) // 2
    length = values.shape[0]
    padded = jnp.pad(values, ((center, center), (0, 0)))
    padded_labels = jnp.pad(labels, (center, center), constant_values=-1)
    rows_list = []
    for tap_index in range(KERNEL):
        matches = (padded_labels[tap_index : tap_index + length] == labels)[:, None]
        taken = grads * padded[tap_index : tap_index + length]
        rows_list.append(jnp.sum(jnp.where(matches, taken, jnp.zeros_like(taken)), axis=0))
    return jnp.stack(rows_list, 0)


def per_device(
    frames, lengths, destinations, offsets, in_weight, depth_weight, out_weight, cotangent
):
    dp_count = lax.axis_size(DP)
    src_rows = frames.shape[0]
    features = frames.shape[1]
    slot_rows = src_rows // dp_count
    entries = lengths.shape[1]
    lengths_row = lengths[0]
    end_rows = jnp.cumsum(lengths_row, dtype=jnp.int32)
    begins = end_rows - lengths_row
    row_ids = jnp.arange(src_rows, dtype=jnp.int32)
    owner_table = (begins[None, :] <= row_ids[:, None]) & (row_ids[:, None] < end_rows[None, :])
    occupied_rows = jnp.any(owner_table, axis=1)

    def lookup(table):
        return jnp.sum(jnp.where(owner_table, table[None, :], 0), axis=1, dtype=jnp.int32)

    entry_ids = jnp.arange(entries, dtype=jnp.int32)
    owner = lookup(entry_ids)
    target = lookup(offsets[0] - begins) + row_ids + 1
    block_ids = jnp.arange(dp_count, dtype=jnp.int32)
    block_dest = jnp.where(occupied_rows, lookup(destinations[0]), -1)[::slot_rows]
    chosen = block_dest[None, :] == block_ids[:, None]
    block_of = jnp.where(
        jnp.any(chosen, axis=1), jnp.sum(jnp.where(chosen, block_ids[None, :], 0), axis=1), dp_count
    )
    codes = jnp.stack((jnp.where(occupied_rows, target, 0), owner), axis=1).astype(frames.dtype)
    blocks = jnp.concatenate((frames, codes), axis=1)
    blocks = jnp.concatenate((blocks, jnp.zeros((slot_rows, features + 2), frames.dtype)), axis=0)
    send = jnp.take(
        blocks.reshape(dp_count + 1, slot_rows, features + 2), block_of, axis=0, mode="clip"
    )
    got = lax.all_to_all(send, DP, split_axis=0, concat_axis=0, tiled=True)
    got = got.reshape(dp_count * slot_rows, features + 2)
    got_target = got[:, features].astype(jnp.int32) - 1
    got_label = (row_ids // slot_rows) * entries + got[:, features + 1].astype(jnp.int32)
    place = got_target[None, :] == jnp.arange(ROWS, dtype=jnp.int32)[:, None]
    packed = jnp.dot(
        place.astype(frames.dtype), got[:, :features], preferred_element_type=jnp.float32
    ).astype(frames.dtype)
    packed_labels = jnp.max(jnp.where(place, got_label[None, :], -1), axis=1)
    hidden = jnp.dot(packed, in_weight, preferred_element_type=jnp.float32).astype(jnp.bfloat16)
    hidden_wide = hidden.astype(jnp.float32)
    taps = depth_weight.astype(jnp.float32)
    convolved = depth_conv(hidden_wide, taps, packed_labels, 1)
    activated = jax.nn.silu(convolved).astype(jnp.bfloat16)
    partial_sum = lax.dot_general(
        activated, out_weight, (((1,), (1,)), ((), ())), preferred_element_type=jnp.float32
    )
    mp_count = lax.axis_size("mp")
    width = out_weight.shape[1]
    block_sums = partial_sum.astype(jnp.bfloat16).reshape(ROWS, mp_count, width)
    branch_parts = lax.all_to_all(
        jnp.swapaxes(block_sums, 0, 1), "mp", split_axis=0, concat_axis=0, tiled=True
    )
    branch = jnp.sum(branch_parts.astype(jnp.float32), axis=0)
    output = (hidden_wide + branch).astype(jnp.bfloat16)
    model_index = lax.axis_index("mp")
    shifted = [cotangent] + [
        lax.ppermute(cotangent, "mp", [(m, (m + k) % mp_count) for m in range(mp_count)])
        for k in range(1, mp_count)
    ]
    order = (model_index - jnp.arange(mp_count, dtype=jnp.int32)) % mp_count
    cotangent_blocks = jnp.take(jnp.stack(shifted, axis=0), order, axis=0, mode="clip")
    weight_blocks = out_weight.reshape(mp_count, width, width)
    grad_scale = 1.0 / math.sqrt(dp_count * ROWS)
    grad_activated = jnp.einsum(
        "mtc,mci->ti", cotangent_blocks, weight_blocks, preferred_element_type=jnp.float32
    )
    sigmoid_value = jax.nn.sigmoid(convolved)
    grad_convolved = grad_activated * sigmoid_value * (1.0 + convolved * (1.0 - sigmoid_value))
    grad_hidden = (
        cotangent.astype(jnp.float32) + depth_conv(grad_convolved, taps, packed_labels, -1)
    ).astype(jnp.bfloat16)
    term_out = grad_scale * jnp.einsum(
        "mtc,ti->mci", cotangent_blocks, activated, preferred_element_type=jnp.float32
    )
    term_in = grad_scale * lax.dot_general(
        packed, grad_hidden, (((0,), (0,)), ((), ())), preferred_element_type=jnp.float32
    )
    term_depth = grad_scale * tap_sums(grad_convolved, hidden_wide, packed_labels)
    out_rows = term_out.shape[0] * term_out.shape[1] // dp_count
    small = jnp.concatenate((term_in, term_depth), axis=0)
    small_rows = -(-small.shape[0] // dp_count)
    small = jnp.pad(small, ((0, small_rows * dp_count - small.shape[0]), (0, 0)))
    combined = jnp.concatenate(
        (
            term_out.reshape(dp_count, out_rows, width),
            small.reshape(dp_count, small_rows, width),
        ),
        axis=1,
    )
    core = lax.axis_index(DP[-1])
    cores = lax.axis_size(DP[-1])
    paired = combined.reshape((dp_count // cores, cores) + combined.shape[1:])
    keep = lax.dynamic_index_in_dim(paired, core, 1, keepdims=False)
    give = lax.dynamic_index_in_dim(paired, 1 - core, 1, keepdims=False)
    pair_sum = keep + lax.ppermute(give, DP[-1], [(0, 1), (1, 0)])
    exchanged = lax.all_to_all(pair_sum, DP[:-1], split_axis=0, concat_axis=0, tiled=True)
    reduced = jnp.sum(exchanged, axis=0)
    out_weight_gradient = reduced[:out_rows]
    spread = jnp.broadcast_to(
        reduced[out_rows:].astype(jnp.bfloat16)[None], (dp_count, small_rows, width)
    )
    gathered = lax.all_to_all(spread, DP, split_axis=0, concat_axis=0, tiled=True)
    small_full = gathered.reshape(dp_count * small_rows, width).astype(jnp.float32)
    in_rows = term_in.shape[0]
    in_weight_gradient = small_full[:in_rows]
    depth_gradient = small_full[in_rows : in_rows + term_depth.shape[0]]
    return (output, in_weight_gradient, depth_gradient, out_weight_gradient)


def split_mesh(mesh):
    devices = mesh.devices
    column = devices[:, 0]
    ys = len({device.coords[1] for device in column})
    zs = len({device.coords[2] for device in column})
    cores = devices.shape[0] // (ys * zs)
    return jax.sharding.Mesh(devices.reshape(ys, zs, cores, devices.shape[1]), DP + ("mp",))


def solution(mesh):
    placed = (
        P(DP, None),
        P(DP, None),
        P(DP, None),
        P(DP, None),
        P(None, "mp"),
        P(None, "mp"),
        P(None, "mp"),
        P(DP, "mp"),
    )
    return jax.shard_map(
        per_device,
        mesh=split_mesh(mesh),
        in_specs=placed,
        out_specs=(P(DP, "mp"), P(None, "mp"), P(None, "mp"), P(DP, "mp")),
        check_vma=False,
    )
```
